128 devices in a mesh: row: 4 (over x_lo, core), col: 32 (over y, x_hi, z).
Axes of the slice: x: 4 (x_hi: 2, x_lo: 2; x = x_hi * 2 + x_lo), y: 4, z: 4, core: 2. Of those that a mesh axis runs over, the one named last changes fastest.
Arguments:
- tokens: bfloat16 [8192, 2048], P('col', 'row'), may hold values from -40 to 40
- router: bfloat16 [2048, 64], replicated, may hold values from -0.375 to 0.375
- expert_ids: int32 [8192, 6], P('col'), may hold values from 0 to 63, all different within a row; in each aligned block of 256 rows (0 to 255, 256 to 511, ...) at most 32 rows name the same one
- expert_in: bfloat16 [64, 2, 2048, 1408], P('col', None, None, 'row'), may hold values from -0.125 to 0.125
- expert_out: bfloat16 [64, 1408, 2048], P('col', 'row'), may hold values from -0.15625 to 0.15625
- shared_in: bfloat16 [2, 2048, 2816], P(None, 'col', 'row'), may hold values from -0.125 to 0.125
- shared_out: bfloat16 [2816, 2048], P('row', 'col'), may hold values from -0.109375 to 0.109375
- kv_cache: bfloat16 [2, 2, 2, 32, 512, 2048], P(None, None, None, 'col', None, 'row'), may hold values from -6 to 6
- lengths: int32 [2], replicated, may hold values from 128 to 16384, as said below
- kv_proj: bfloat16 [2048, 2, 2048], P(None, None, 'row'), may hold values from -0.125 to 0.125
Outputs:
- mixed_out: bfloat16 [8192, 2048], P('col', 'row')
- cache_out: bfloat16 [2, 2, 2, 32, 512, 2048], P(None, None, None, None, ('row', 'col'))
The draws below stay inside these ranges and needn't reach their ends.
Inputs may be any that keep to these rules, and one draw needn't show every extreme that they name: `expert_ids`: each token names 6 different experts; among the 256 tokens of one aligned block no expert is named by more than 32 tokens, and in some blocks one is named by exactly 32. `lengths`: exactly 1 entries are 16384; each other entry is at least 128 and at most 256.
All inputs are finite; a program needn't handle non-finite values.
Results may differ from the reference program's by a relative error of at most 0.013.
Values may be sent and summed in bfloat16 or wider, within the bound.
No kernel may reach another device: no remote copies, remote signals or barrier semaphores. Data moves between devices by JAX's collectives and lax.ppermute only.
A program may use at most 128 MiB of HBM per device.

```python
import math
import jax
import jax.numpy as jnp
import numpy as np
from jax import lax

D = 2048
FF = 1408
EXPERTS = 64
TOP = 6
LKV = 2
CTX = 16384
SHORT = 256
TOK_DEV = 256
REQ = 2
CAP = 32
TOKENS = 8192
BLOCKS = 32
FF_PARTS = 4
SFF = 2816
HF = 2048
SLABS = 32
CSL = 512


def draw_tokens(key, part):
    first, second, third = jax.random.split(key, 3)
    column_scale = jnp.exp(jax.random.uniform(third, (1, D), jnp.float32, -0.7, 0.7))
    row_scale = jnp.exp(jax.random.uniform(second, (TOKENS, 1), jnp.float32, -1.2, 1.2))
    base = jnp.clip(jax.random.normal(first, (TOKENS, D), jnp.float32), -5.0, 5.0)
    values = jnp.clip(base * row_scale * column_scale, -40.0, 40.0)
    return values.astype(jnp.bfloat16)


def draw_lengths(key, part):
    ranks = jax.random.permutation(jax.random.fold_in(key, 7), REQ).astype(jnp.int32)
    short_values = jax.random.randint(jax.random.fold_in(key, 11), (REQ,), SHORT // 2, SHORT + 1, jnp.int32)
    return jnp.where(ranks < REQ // 2, CTX, short_values).astype(jnp.int32)


def block_levels(stream_key, dims, cuts, low, high):
    def one(dim, shards_of):
        steps = jax.random.uniform(jax.random.fold_in(jax.random.fold_in(stream_key, 6), dim), (shards_of,), jnp.float32, low / len(cuts), high / len(cuts))
        return jnp.repeat(jnp.exp(steps), dims[dim] // shards_of).reshape((-1,) + (1,) * (len(dims) - dim - 1))

    level = one(*cuts[0])
    for cut in cuts[1:]:
        level = level * one(*cut)
    return level


def routed_block(stream_key, own, number, rows, number_of, top, bound, skew):
    order = jax.random.permutation(stream_key, number_of)
    heavy_load, ordinary = load_shares(number_of, rows * top, bound, skew, True), load_shares(number_of, rows * top, bound, skew, False)
    places = jnp.arange(number_of)

    def named(sizes, rotation):
        used = int((sizes > 0).sum())
        fixed = max(1, used // 4)
        moved = fixed + (places - fixed + rotation * (used - fixed)) % max(1, number_of - fixed)
        return jnp.zeros((number_of,), jnp.int32).at[order[jnp.where(places < fixed, places, moved)]].set(jnp.asarray(sizes, jnp.int32))

    sizes = jnp.where(number % 4 == 0, named(heavy_load, number // 4), named(ordinary, number - number // 4 - 1))
    mixed = jax.random.permutation(jax.random.fold_in(own, 3), number_of)
    source_of, sink = mixed[0:number_of // 2 * 2:2], mixed[1:number_of // 2 * 2:2]
    room = jnp.minimum(sizes[source_of] - 1, bound - sizes[sink]) // 2
    room = jnp.where((source_of == order[0]) | (sink == order[0]) | (sizes[sink] == 0), 0, jnp.maximum(room, 0))
    moved = jax.random.randint(jax.random.fold_in(own, 4), (number_of // 2,), 0, 1 << 20) % (room + 1)
    sizes = sizes.at[source_of].add(-moved).at[sink].add(moved)
    items = jnp.searchsorted(jnp.cumsum(sizes), jnp.arange(rows * top), side="right").astype(jnp.int32)
    listing = items.reshape(top, rows).T
    listing = listing[jax.random.permutation(jax.random.fold_in(own, 1), rows)]
    rotation = jax.random.randint(jax.random.fold_in(own, 2), (rows, 1), 0, top)
    return jnp.take_along_axis(listing, (jnp.arange(top)[None, :] + rotation) % top, axis=1)


def load_shares(number_of, total, most, lean, full):
    loads = [(1 << 20) // math.isqrt(rank ** lean) + 1 for rank in range(1, number_of + 1)]
    largest = most if full else min(most, max(-(-total // number_of), total * loads[0] // sum(loads)))
    least = 1 if total - largest >= number_of - 1 else 0
    holding, surplus = [largest] + [least] * (number_of - 1), total - largest - least * (number_of - 1)
    while surplus > 0:
        movable = [i for i in range(1, number_of) if holding[i] < largest] or [i for i in range(1, number_of) if holding[i] < most]
        pool, left = sum([loads[i] for i in movable]), surplus
        for i in movable:
            addition = min(most - holding[i], max(1, left * loads[i] // pool), surplus)
            holding[i] = holding[i] + addition
            surplus = surplus - addition
    return np.array(holding)


def noise(rng, dims, deviation, bound, cuts=(), kind=jnp.bfloat16):
    result = jax.random.normal(rng, dims, jnp.float32) * deviation
    if len(cuts) > 0:
        result = block_levels(rng, dims, cuts, -0.22, 0.18) * result
    return jnp.clip(result, min=-bound, max=bound).astype(kind)


def setup_inputs(seed: int = 0) -> dict:
    seeds = jax.random.split(jax.random.key(seed), 11)
    tokens = draw_tokens(jax.random.fold_in(seeds[10], 71), 0)
    router = noise(seeds[1], (D, EXPERTS), (D // 9) ** -0.5, 0.375)
    expert_ids_keys = jax.random.split(jax.random.fold_in(seeds[2], 1), TOKENS // TOK_DEV)
    expert_ids_turns = jax.random.permutation(jax.random.fold_in(seeds[2], 3), TOKENS // TOK_DEV)
    expert_ids = jax.vmap(lambda own, number: routed_block(jax.random.fold_in(seeds[2], 2), own, number, TOK_DEV, EXPERTS, TOP, CAP, 1))(expert_ids_keys, expert_ids_turns).reshape((TOKENS, TOP))
    expert_in = noise(seeds[3], (EXPERTS, 2, D, FF), D ** -0.5, 0.125, ((0, 32), (3, 4)))
    expert_out = noise(seeds[4], (EXPERTS, FF, D), FF ** -0.5, 0.15625, ((0, 32), (1, 4)))
    shared_in = noise(seeds[5], (2, D, SFF), D ** -0.5, 0.125, ((1, 32), (2, 4)))
    shared_out = noise(seeds[6], (SFF, D), SFF ** -0.5, 0.109375, ((0, 4), (1, 32)))
    kv_cache = noise(seeds[7], (LKV, 2, REQ, SLABS, CSL, HF), 1.0, 6.0, ((3, 32), (5, 4)))
    lengths = draw_lengths(jax.random.fold_in(seeds[10], 71), 0)
    kv_proj = noise(seeds[9], (D, 2, HF), D ** -0.5, 0.125, ((2, 4),))
    return dict(tokens=tokens, router=router, expert_ids=expert_ids, expert_in=expert_in, expert_out=expert_out, shared_in=shared_in, shared_out=shared_out, kv_cache=kv_cache, lengths=lengths, kv_proj=kv_proj)


def reference(tokens, router, expert_ids, expert_in, expert_out, shared_in, shared_out, kv_cache, lengths, kv_proj):
    tokens_f = tokens.astype(jnp.float32)
    normed = (tokens_f * lax.rsqrt(lax.optimization_barrier(jnp.mean(tokens_f * tokens_f, axis=-1, keepdims=True)) + 1e-06)).astype(jnp.bfloat16)
    logits = jnp.dot(normed, router, preferred_element_type=jnp.float32)
    picked = jnp.take_along_axis(logits, expert_ids, axis=1)
    sigmoids = jax.nn.sigmoid(picked)
    gate_weights = sigmoids / lax.optimization_barrier(jnp.sum(sigmoids, axis=1, keepdims=True))
    blocks = expert_ids.reshape(BLOCKS, TOK_DEV * TOP)
    catalog = jnp.arange(EXPERTS, dtype=jnp.int32)
    onehot = (blocks[:, :, None] == catalog).astype(jnp.int32)
    position = lax.optimization_barrier(jnp.sum(onehot * (jnp.cumsum(onehot, axis=1) - 1), axis=2)).astype(jnp.int32)
    slot_rows = (jnp.arange(BLOCKS, dtype=jnp.int32)[:, None] * CAP + position).astype(jnp.int32)
    token_index = (jnp.arange(TOKENS * TOP, dtype=jnp.int32) // TOP).reshape(BLOCKS, TOK_DEV * TOP)
    source = jnp.full((EXPERTS, BLOCKS * CAP), -1, jnp.int32).at[blocks, slot_rows].set(token_index)

    def run_expert(package):
        weights_in, weights_out, source_rows = package
        buffer = jnp.where((source_rows >= 0)[:, None], normed[jnp.maximum(source_rows, 0)], jnp.zeros((), normed.dtype))
        gate_act = jnp.dot(buffer, weights_in[0], preferred_element_type=jnp.float32)
        up_act = jnp.dot(buffer, weights_in[1], preferred_element_type=jnp.float32)
        hidden = (jax.nn.silu(gate_act) * up_act).astype(jnp.bfloat16)
        hidden_blocks = hidden.reshape(BLOCKS * CAP, FF_PARTS, FF // FF_PARTS).astype(jnp.float32)
        weight_blocks = weights_out.reshape(FF_PARTS, FF // FF_PARTS, D).astype(jnp.float32)
        partial_sums = jnp.einsum('rbf,bfd->rbd', hidden_blocks, weight_blocks)
        partial_sums = lax.optimization_barrier(partial_sums.astype(jnp.bfloat16)).astype(jnp.float32)
        return lax.optimization_barrier(jnp.sum(partial_sums, axis=1)).astype(jnp.bfloat16)
    expert_result = lax.map(run_expert, (expert_in, expert_out, source))
    routed = expert_result[expert_ids.reshape(-1), slot_rows.reshape(-1)].reshape(TOKENS, TOP, D).astype(jnp.float32)
    routed_sum = lax.optimization_barrier(jnp.sum(gate_weights[:, :, None] * routed, axis=1))
    shared_gate = jnp.dot(normed, shared_in[0], preferred_element_type=jnp.float32)
    shared_up = jnp.dot(normed, shared_in[1], preferred_element_type=jnp.float32)
    shared_hidden = (jax.nn.silu(shared_gate) * shared_up).astype(jnp.bfloat16)
    shared_part = jnp.dot(shared_hidden, shared_out, preferred_element_type=jnp.float32)
    mixed_out = (shared_part + routed_sum).astype(jnp.bfloat16)
    span_kv = jnp.einsum('td,dph->tph', normed.astype(jnp.float32), kv_proj.astype(jnp.float32)).astype(jnp.bfloat16)
    first_long = jnp.min(jnp.where(lengths == CTX, jnp.arange(REQ, dtype=jnp.int32), REQ)).astype(jnp.int32)
    places = jnp.arange(SLABS, dtype=jnp.int32)[:, None] * CSL + jnp.arange(CSL, dtype=jnp.int32)[None, :]
    live_mask = places[None, :, :] < lengths[:, None, None]
    cache_out = jnp.where(live_mask[None, None, :, :, :, None], kv_cache, jnp.zeros((), kv_cache.dtype))
    flat_cache = cache_out.reshape(LKV, 2, REQ, CTX, HF)
    flat_cache = flat_cache.at[LKV - 1, :, first_long, CTX - TOKENS:, :].set(span_kv.transpose(1, 0, 2))
    cache_out = flat_cache.reshape(LKV, 2, REQ, SLABS, CSL, HF)
    return (mixed_out, cache_out)
```

```python
import jax
import jax.numpy as jnp
from jax import lax
from jax.sharding import Mesh
from jax.sharding import PartitionSpec as P

CTX = 16384
CAP = 32
ROW = ("xl", "core")
COL = ("y", "xh", "z")
AXES = ROW + COL


def relay_slabs(chosen, row_count, col_count):
    layers = chosen.shape[0]
    pairs = chosen.shape[1]
    requests = chosen.shape[2]
    slab_len = chosen.shape[4]
    head_width = chosen.shape[5]
    groups = layers * pairs * requests
    sectioned = chosen.reshape(groups, 1, slab_len, head_width)
    piece_len = slab_len // (row_count * col_count)
    relaid = lax.all_to_all(sectioned, AXES, split_axis=2, concat_axis=1, tiled=True)
    relaid = relaid.reshape(groups, row_count, col_count, piece_len, head_width)
    relaid = relaid.transpose(0, 2, 3, 1, 4).reshape(
        groups, col_count, piece_len, row_count * head_width
    )
    return relaid.reshape(layers, pairs, requests, col_count, piece_len, row_count * head_width)


def row_order(x, dim):
    shape = x.shape
    quarter = shape[dim] // 4
    split = x.reshape(shape[:dim] + (2, 2, quarter) + shape[dim + 1 :])
    return jnp.swapaxes(split, dim, dim + 1).reshape(shape)


def row_reduce_scatter(x, dim):
    half = lax.psum_scatter(x, "core", scatter_dimension=dim, tiled=True)
    return lax.psum_scatter(half, "xl", scatter_dimension=dim, tiled=True)


def col_gather(x, dim):
    for name in ("z", "xh", "y"):
        x = lax.all_gather(x, name, axis=dim, tiled=True)
    return x


def local(
    tokens,
    router,
    expert_ids,
    expert_in,
    expert_out,
    shared_in,
    shared_out,
    kv_cache,
    lengths,
    kv_proj,
    row_count,
    col_count,
):
    row_index = lax.axis_index(ROW)
    col_index = lax.axis_index(COL)
    core_index = lax.axis_index("core")
    tok_rows = tokens.shape[0]
    slice_width = tokens.shape[1]
    gathered = lax.all_gather(tokens, "core", axis=1, tiled=True)
    gathered = lax.all_gather(gathered, "xl", axis=1, tiled=True)
    width = gathered.shape[1]
    half_width = width // 2
    tokens_f = gathered.astype(jnp.float32)
    normed = (
        tokens_f * lax.rsqrt(jnp.mean(tokens_f * tokens_f, axis=-1, keepdims=True) + 1e-06)
    ).astype(jnp.bfloat16)
    logits = jnp.dot(normed, router, preferred_element_type=jnp.float32)
    expert_total = router.shape[1]
    top_count = expert_ids.shape[1]
    catalog = jnp.arange(expert_total, dtype=jnp.int32)
    matches = expert_ids[:, :, None] == catalog
    picked = jnp.sum(jnp.where(matches, logits[:, None, :], 0.0), axis=2)
    sigmoids = jax.nn.sigmoid(picked)
    gate_weights = sigmoids / jnp.sum(sigmoids, axis=1, keepdims=True)
    flat_ids = expert_ids.reshape(-1)
    pair_count = flat_ids.shape[0]
    onehot = (flat_ids[:, None] == catalog).astype(jnp.bfloat16)
    pair_iota = jnp.arange(pair_count, dtype=jnp.int32)
    earlier = (pair_iota[None, :] < pair_iota[:, None]).astype(jnp.bfloat16)
    before = jnp.dot(earlier, onehot, preferred_element_type=jnp.float32)
    slot_index = jnp.sum(before * onehot.astype(jnp.float32), axis=1).astype(jnp.int32)
    dest_index = flat_ids * CAP + slot_index
    slot_total = expert_total * CAP
    slots = jnp.arange(slot_total, dtype=jnp.int32)
    dest_tok = dest_index.reshape(tok_rows, top_count)
    select_tok = jnp.any(dest_tok[None, :, :] == slots[:, None, None], axis=2).astype(jnp.bfloat16)
    local_experts = expert_total // col_count
    own_half = lax.dynamic_slice_in_dim(normed, core_index * half_width, half_width, axis=1)
    outgoing = jnp.dot(select_tok, own_half, preferred_element_type=jnp.float32)
    outgoing = outgoing.astype(jnp.bfloat16).reshape(col_count, local_experts, CAP, half_width)
    incoming_own = lax.all_to_all(outgoing, COL, split_axis=0, concat_axis=0, tiled=True)
    incoming_other = lax.ppermute(incoming_own, "core", perm=[(0, 1), (1, 0)])
    weights_own = lax.dynamic_slice_in_dim(expert_in, core_index * half_width, half_width, axis=2)
    weights_other = lax.dynamic_slice_in_dim(
        expert_in, (1 - core_index) * half_width, half_width, axis=2
    )
    gate_up = jnp.einsum(
        "secd,egdf->gsecf", incoming_own, weights_own, preferred_element_type=jnp.float32
    ) + jnp.einsum(
        "secd,egdf->gsecf", incoming_other, weights_other, preferred_element_type=jnp.float32
    )
    hidden = (jax.nn.silu(gate_up[0]) * gate_up[1]).astype(jnp.bfloat16)
    partial_out = jnp.einsum(
        "secf,efd->secd", hidden, row_order(expert_out, 2), preferred_element_type=jnp.float32
    )
    summed = row_reduce_scatter(partial_out.astype(jnp.bfloat16), 3)
    returned = lax.all_to_all(summed, COL, split_axis=0, concat_axis=0, tiled=True).reshape(
        slot_total, slice_width
    )
    pick = (dest_index[:, None] == slots[None, :]).astype(jnp.bfloat16)
    routed = jnp.dot(pick, returned, preferred_element_type=jnp.float32)
    routed = routed.reshape(tok_rows, top_count, slice_width)
    routed_sum = jnp.sum(gate_weights[:, :, None] * routed, axis=1)
    shared_acc = jnp.einsum(
        "td,gdf->gtf",
        normed,
        col_gather(shared_in, 1),
        preferred_element_type=jnp.float32,
    )
    shared_hidden = (jax.nn.silu(shared_acc[0]) * shared_acc[1]).astype(jnp.bfloat16)
    shared_terms = jnp.dot(
        shared_hidden,
        row_order(col_gather(shared_out, 1), 1),
        preferred_element_type=jnp.float32,
    )
    shared_part = row_reduce_scatter(shared_terms.astype(jnp.bfloat16), 1).astype(jnp.float32)
    mixed_out = (shared_part + routed_sum).astype(jnp.bfloat16)
    layers = kv_cache.shape[0]
    pairs = kv_cache.shape[1]
    requests = kv_cache.shape[2]
    slab_len = kv_cache.shape[4]
    head_slice = kv_cache.shape[5]
    piece_len = slab_len // (row_count * col_count)
    device_total = row_count * col_count
    span_local = jnp.einsum(
        "td,dph->tph", normed, kv_proj, preferred_element_type=jnp.float32
    ).astype(jnp.bfloat16)
    first_pos = CTX - tok_rows * col_count
    send_offset = (first_pos + col_index * tok_rows) % slab_len
    outbound = lax.dynamic_update_slice(
        jnp.zeros((slab_len, pairs, head_slice), jnp.bfloat16), span_local, (send_offset, 0, 0)
    )
    outbound = outbound.reshape(device_total, piece_len, pairs, head_slice)
    inbound = lax.all_to_all(outbound, AXES, split_axis=0, concat_axis=0, tiled=True)
    inbound = inbound.reshape(row_count, col_count, piece_len, pairs, head_slice)
    device_flat = row_index * col_count + col_index
    source_block = jnp.arange(col_count, dtype=jnp.int32)[:, None]
    within = device_flat * piece_len + jnp.arange(piece_len, dtype=jnp.int32)[None, :]
    offset_tok = (within - first_pos - source_block * tok_rows) % slab_len
    usable = offset_tok < tok_rows
    slab_of = (first_pos + source_block * tok_rows + offset_tok) // slab_len
    slab_ids = jnp.arange(col_count, dtype=jnp.int32)[:, None, None]
    placing = ((slab_of[None, :, :] == slab_ids) & usable[None, :, :]).astype(jnp.bfloat16)
    placed = jnp.einsum("sck,rckph->pskrh", placing, inbound, preferred_element_type=jnp.float32)
    placed = placed.reshape(pairs, col_count, piece_len, row_count * head_slice).astype(
        jnp.bfloat16
    )
    covered = jnp.sum(placing.astype(jnp.float32), axis=1) > 0.5
    first_long = jnp.min(jnp.where(lengths == CTX, jnp.arange(requests, dtype=jnp.int32), requests))
    relaid = relay_slabs(kv_cache, row_count, col_count)
    start_pos = (row_index * col_count + col_index) * piece_len
    places = (
        jnp.arange(col_count, dtype=jnp.int32)[:, None] * slab_len
        + start_pos
        + jnp.arange(piece_len, dtype=jnp.int32)[None, :]
    )
    live_mask = places[None, :, :] < lengths[:, None, None]
    cache_out = jnp.where(live_mask[None, None, :, :, :, None], relaid, jnp.zeros((), relaid.dtype))
    layer_pick = (jnp.arange(layers, dtype=jnp.int32) == layers - 1)[
        :, None, None, None, None, None
    ]
    request_pick = (jnp.arange(requests, dtype=jnp.int32) == first_long)[
        None, None, :, None, None, None
    ]
    select = layer_pick & request_pick & covered[None, None, None, :, :, None]
    cache_out = jnp.where(select, placed[None, :, None], cache_out)
    return (mixed_out, cache_out)


def solution(mesh):
    row_count = mesh.shape["row"]
    col_count = mesh.shape["col"]
    fine = Mesh(mesh.devices.reshape(2, row_count // 2, 4, 2, col_count // 8), AXES)

    def body(*args):
        return local(*args, row_count, col_count)

    return jax.shard_map(
        body,
        mesh=fine,
        in_specs=(
            P(COL, ROW),
            P(),
            P(COL, None),
            P(COL, None, None, ROW),
            P(COL, ROW, None),
            P(None, COL, ROW),
            P(ROW, COL),
            P(None, None, None, COL, None, ROW),
            P(),
            P(None, None, ROW),
        ),
        out_specs=(P(COL, ROW), P(None, None, None, None, AXES, None)),
        check_vma=False,
    )
```

```python
import jax
import jax.numpy as jnp
from jax import lax
from jax.sharding import Mesh
from jax.sharding import PartitionSpec as P

CTX = 16384
CAP = 32
ROW = ("xl", "core")
COL = ("y", "xh", "z")
AXES = ROW + COL


def relay_slabs(chosen, row_count, col_count):
    layers = chosen.shape[0]
    pairs = chosen.shape[1]
    requests = chosen.shape[2]
    slab_len = chosen.shape[4]
    head_width = chosen.shape[5]
    groups = layers * pairs * requests
    sectioned = chosen.reshape(groups, 1, slab_len, head_width)
    piece_len = slab_len // (row_count * col_count)
    relaid = lax.all_to_all(sectioned, AXES, split_axis=2, concat_axis=1, tiled=True)
    relaid = relaid.reshape(groups, row_count, col_count, piece_len, head_width)
    relaid = relaid.transpose(0, 2, 3, 1, 4).reshape(
        groups, col_count, piece_len, row_count * head_width
    )
    return relaid.reshape(layers, pairs, requests, col_count, piece_len, row_count * head_width)


def row_order(x, dim):
    shape = x.shape
    quarter = shape[dim] // 4
    split = x.reshape(shape[:dim] + (2, 2, quarter) + shape[dim + 1 :])
    return jnp.swapaxes(split, dim, dim + 1).reshape(shape)


def swap_gather(x, name, index):
    other = lax.ppermute(x, name, perm=[(0, 1), (1, 0)])
    return jnp.where(
        index == 0, jnp.concatenate([x, other], axis=-1), jnp.concatenate([other, x], axis=-1)
    )


def swap_reduce(x, name, index, dim):
    block = x.shape[dim] // 2
    keep = lax.dynamic_slice_in_dim(x, index * block, block, axis=dim)
    give = lax.dynamic_slice_in_dim(x, (1 - index) * block, block, axis=dim)
    got = lax.ppermute(give, name, perm=[(0, 1), (1, 0)])
    return keep.astype(jnp.float32) + got.astype(jnp.float32)


def col_gather(x, dim):
    for name in ("z", "xh", "y"):
        x = lax.all_gather(x, name, axis=dim, tiled=True)
    return x


def local(
    tokens,
    router,
    expert_ids,
    expert_in,
    expert_out,
    shared_in,
    shared_out,
    kv_cache,
    lengths,
    kv_proj,
    row_count,
    col_count,
):
    row_index = lax.axis_index(ROW)
    col_index = lax.axis_index(COL)
    core_index = lax.axis_index("core")
    tok_rows = tokens.shape[0]
    slice_width = tokens.shape[1]
    xl_index = lax.axis_index("xl")
    gathered = swap_gather(tokens, "core", core_index)
    gathered = swap_gather(gathered, "xl", xl_index)
    width = gathered.shape[1]
    half_width = width // 2
    tokens_f = gathered.astype(jnp.float32)
    normed = (
        tokens_f * lax.rsqrt(jnp.mean(tokens_f * tokens_f, axis=-1, keepdims=True) + 1e-06)
    ).astype(jnp.bfloat16)
    logits = jnp.dot(normed, router, preferred_element_type=jnp.float32)
    expert_total = router.shape[1]
    top_count = expert_ids.shape[1]
    catalog = jnp.arange(expert_total, dtype=jnp.int32)
    matches = expert_ids[:, :, None] == catalog
    picked = jnp.sum(jnp.where(matches, logits[:, None, :], 0.0), axis=2)
    sigmoids = jax.nn.sigmoid(picked)
    gate_weights = sigmoids / jnp.sum(sigmoids, axis=1, keepdims=True)
    flat_ids = expert_ids.reshape(-1)
    pair_count = flat_ids.shape[0]
    onehot = (flat_ids[:, None] == catalog).astype(jnp.bfloat16)
    pair_iota = jnp.arange(pair_count, dtype=jnp.int32)
    earlier = (pair_iota[None, :] < pair_iota[:, None]).astype(jnp.bfloat16)
    before = jnp.dot(earlier, onehot, preferred_element_type=jnp.float32)
    slot_index = jnp.sum(before * onehot.astype(jnp.float32), axis=1).astype(jnp.int32)
    dest_index = flat_ids * CAP + slot_index
    slot_total = expert_total * CAP
    slots = jnp.arange(slot_total, dtype=jnp.int32)
    dest_tok = dest_index.reshape(tok_rows, top_count)
    select_tok = jnp.any(dest_tok[None, :, :] == slots[:, None, None], axis=2).astype(jnp.bfloat16)
    local_experts = expert_total // col_count
    own_half = lax.dynamic_slice_in_dim(normed, core_index * half_width, half_width, axis=1)
    outgoing = jnp.dot(select_tok, own_half, preferred_element_type=jnp.float32)
    outgoing = outgoing.astype(jnp.bfloat16).reshape(col_count, local_experts, CAP, half_width)
    incoming_own = lax.all_to_all(outgoing, COL, split_axis=0, concat_axis=0, tiled=True)
    incoming_other = lax.ppermute(incoming_own, "core", perm=[(0, 1), (1, 0)])
    weights_own = lax.dynamic_slice_in_dim(expert_in, core_index * half_width, half_width, axis=2)
    weights_other = lax.dynamic_slice_in_dim(
        expert_in, (1 - core_index) * half_width, half_width, axis=2
    )
    gate_up = jnp.einsum(
        "secd,egdf->gsecf", incoming_own, weights_own, preferred_element_type=jnp.float32
    ) + jnp.einsum(
        "secd,egdf->gsecf", incoming_other, weights_other, preferred_element_type=jnp.float32
    )
    hidden = (jax.nn.silu(gate_up[0]) * gate_up[1]).astype(jnp.bfloat16)
    partial_out = jnp.einsum(
        "secf,efd->secd", hidden, row_order(expert_out, 2), preferred_element_type=jnp.float32
    )
    chip_sum = swap_reduce(partial_out.astype(jnp.bfloat16), "core", core_index, 3)
    send = chip_sum.astype(jnp.bfloat16).reshape(col_count, local_experts, CAP, 2, slice_width)
    send = send.transpose(3, 0, 1, 2, 4).reshape(2 * col_count, local_experts, CAP, slice_width)
    both = lax.all_to_all(send, ("xl",) + COL, split_axis=0, concat_axis=0, tiled=True)
    both = both.astype(jnp.float32).reshape(2, slot_total, slice_width)
    returned = (both[0] + both[1]).astype(jnp.bfloat16)
    pick = (dest_index[:, None] == slots[None, :]).astype(jnp.bfloat16)
    routed = jnp.dot(pick, returned, preferred_element_type=jnp.float32)
    routed = routed.reshape(tok_rows, top_count, slice_width)
    routed_sum = jnp.sum(gate_weights[:, :, None] * routed, axis=1)
    shared_acc = jnp.einsum(
        "td,gdf->gtf",
        normed,
        col_gather(shared_in, 1),
        preferred_element_type=jnp.float32,
    )
    shared_hidden = (jax.nn.silu(shared_acc[0]) * shared_acc[1]).astype(jnp.bfloat16)
    shared_terms = jnp.dot(
        shared_hidden,
        row_order(col_gather(shared_out, 1), 1),
        preferred_element_type=jnp.float32,
    )
    shared_half = swap_reduce(shared_terms.astype(jnp.bfloat16), "core", core_index, 1)
    shared_part = swap_reduce(shared_half.astype(jnp.bfloat16), "xl", xl_index, 1)
    mixed_out = (shared_part + routed_sum).astype(jnp.bfloat16)
    layers = kv_cache.shape[0]
    pairs = kv_cache.shape[1]
    requests = kv_cache.shape[2]
    slab_len = kv_cache.shape[4]
    head_slice = kv_cache.shape[5]
    piece_len = slab_len // (row_count * col_count)
    device_total = row_count * col_count
    span_local = jnp.einsum(
        "td,dph->tph", normed, kv_proj, preferred_element_type=jnp.float32
    ).astype(jnp.bfloat16)
    first_pos = CTX - tok_rows * col_count
    send_offset = (first_pos + col_index * tok_rows) % slab_len
    outbound = lax.dynamic_update_slice(
        jnp.zeros((slab_len, pairs, head_slice), jnp.bfloat16), span_local, (send_offset, 0, 0)
    )
    outbound = outbound.reshape(device_total, piece_len, pairs, head_slice)
    inbound = lax.all_to_all(outbound, AXES, split_axis=0, concat_axis=0, tiled=True)
    inbound = inbound.reshape(row_count, col_count, piece_len, pairs, head_slice)
    device_flat = row_index * col_count + col_index
    source_block = jnp.arange(col_count, dtype=jnp.int32)[:, None]
    within = device_flat * piece_len + jnp.arange(piece_len, dtype=jnp.int32)[None, :]
    offset_tok = (within - first_pos - source_block * tok_rows) % slab_len
    usable = offset_tok < tok_rows
    slab_of = (first_pos + source_block * tok_rows + offset_tok) // slab_len
    slab_ids = jnp.arange(col_count, dtype=jnp.int32)[:, None, None]
    placing = ((slab_of[None, :, :] == slab_ids) & usable[None, :, :]).astype(jnp.bfloat16)
    placed = jnp.einsum("sck,rckph->pskrh", placing, inbound, preferred_element_type=jnp.float32)
    placed = placed.reshape(pairs, col_count, piece_len, row_count * head_slice).astype(
        jnp.bfloat16
    )
    covered = jnp.sum(placing.astype(jnp.float32), axis=1) > 0.5
    first_long = jnp.min(jnp.where(lengths == CTX, jnp.arange(requests, dtype=jnp.int32), requests))
    relaid = relay_slabs(kv_cache, row_count, col_count)
    start_pos = (row_index * col_count + col_index) * piece_len
    places = (
        jnp.arange(col_count, dtype=jnp.int32)[:, None] * slab_len
        + start_pos
        + jnp.arange(piece_len, dtype=jnp.int32)[None, :]
    )
    live_mask = places[None, :, :] < lengths[:, None, None]
    cache_out = jnp.where(live_mask[None, None, :, :, :, None], relaid, jnp.zeros((), relaid.dtype))
    layer_pick = (jnp.arange(layers, dtype=jnp.int32) == layers - 1)[
        :, None, None, None, None, None
    ]
    request_pick = (jnp.arange(requests, dtype=jnp.int32) == first_long)[
        None, None, :, None, None, None
    ]
    select = layer_pick & request_pick & covered[None, None, None, :, :, None]
    cache_out = jnp.where(select, placed[None, :, None], cache_out)
    return (mixed_out, cache_out)


def solution(mesh):
    row_count = mesh.shape["row"]
    col_count = mesh.shape["col"]
    fine = Mesh(mesh.devices.reshape(2, row_count // 2, 4, 2, col_count // 8), AXES)

    def body(*args):
        return local(*args, row_count, col_count)

    return jax.shard_map(
        body,
        mesh=fine,
        in_specs=(
            P(COL, ROW),
            P(),
            P(COL, None),
            P(COL, None, None, ROW),
            P(COL, ROW, None),
            P(None, COL, ROW),
            P(ROW, COL),
            P(None, None, None, COL, None, ROW),
            P(),
            P(None, None, ROW),
        ),
        out_specs=(P(COL, ROW), P(None, None, None, None, AXES, None)),
        check_vma=False,
    )
```

```python
import jax
import jax.numpy as jnp
from jax import lax
from jax.sharding import Mesh
from jax.sharding import PartitionSpec as P

CTX = 16384
CAP = 32
ROW = ("xl", "core")
COL = ("y", "xh", "z")
AXES = ROW + COL


def relay_slabs(chosen, row_count, col_count):
    layers = chosen.shape[0]
    pairs = chosen.shape[1]
    requests = chosen.shape[2]
    slab_len = chosen.shape[4]
    head_width = chosen.shape[5]
    groups = layers * pairs * requests
    sectioned = chosen.reshape(groups, 1, slab_len, head_width)
    piece_len = slab_len // (row_count * col_count)
    relaid = lax.all_to_all(sectioned, AXES, split_axis=2, concat_axis=1, tiled=True)
    relaid = relaid.reshape(groups, row_count, col_count, piece_len, head_width)
    relaid = relaid.transpose(0, 2, 3, 1, 4).reshape(
        groups, col_count, piece_len, row_count * head_width
    )
    return relaid.reshape(layers, pairs, requests, col_count, piece_len, row_count * head_width)


def row_order(x, dim):
    shape = x.shape
    quarter = shape[dim] // 4
    split = x.reshape(shape[:dim] + (2, 2, quarter) + shape[dim + 1 :])
    return jnp.swapaxes(split, dim, dim + 1).reshape(shape)


def swap_gather(x, name, index):
    other = lax.ppermute(x, name, perm=[(0, 1), (1, 0)])
    return jnp.where(
        index == 0, jnp.concatenate([x, other], axis=-1), jnp.concatenate([other, x], axis=-1)
    )


def swap_reduce(x, name, index, dim):
    block = x.shape[dim] // 2
    keep = lax.dynamic_slice_in_dim(x, index * block, block, axis=dim)
    give = lax.dynamic_slice_in_dim(x, (1 - index) * block, block, axis=dim)
    got = lax.ppermute(give, name, perm=[(0, 1), (1, 0)])
    return keep.astype(jnp.float32) + got.astype(jnp.float32)


def ring_gather(x, name, size):
    if size == 2:
        return jnp.stack([x, lax.ppermute(x, name, perm=[(0, 1), (1, 0)])], axis=0)
    half = x.shape[0] // 2
    fwd, bwd = x[:half], x[half:]
    ahead = [(i, (i + 1) % size) for i in range(size)]
    behind = [(i, (i - 1) % size) for i in range(size)]
    fwd_parts, bwd_parts = [fwd], [bwd]
    for _ in range(1, size):
        fwd = lax.ppermute(fwd, name, perm=ahead)
        bwd = lax.ppermute(bwd, name, perm=behind)
        fwd_parts.append(fwd)
        bwd_parts.append(bwd)
    return jnp.stack(
        [
            jnp.concatenate([fwd_parts[d], bwd_parts[(size - d) % size]], axis=0)
            for d in range(size)
        ],
        axis=0,
    )


def local(
    tokens,
    router,
    expert_ids,
    expert_in,
    expert_out,
    shared_in,
    shared_out,
    kv_cache,
    lengths,
    kv_proj,
    row_count,
    col_count,
):
    row_index = lax.axis_index(ROW)
    col_index = lax.axis_index(COL)
    core_index = lax.axis_index("core")
    tok_rows = tokens.shape[0]
    slice_width = tokens.shape[1]
    xl_index = lax.axis_index("xl")
    gathered = swap_gather(tokens, "core", core_index)
    gathered = swap_gather(gathered, "xl", xl_index)
    width = gathered.shape[1]
    half_width = width // 2
    tokens_f = gathered.astype(jnp.float32)
    normed = (
        tokens_f * lax.rsqrt(jnp.mean(tokens_f * tokens_f, axis=-1, keepdims=True) + 1e-06)
    ).astype(jnp.bfloat16)
    logits = jnp.dot(normed, router, preferred_element_type=jnp.float32)
    expert_total = router.shape[1]
    top_count = expert_ids.shape[1]
    catalog = jnp.arange(expert_total, dtype=jnp.int32)
    matches = expert_ids[:, :, None] == catalog
    picked = jnp.sum(jnp.where(matches, logits[:, None, :], 0.0), axis=2)
    sigmoids = jax.nn.sigmoid(picked)
    gate_weights = sigmoids / jnp.sum(sigmoids, axis=1, keepdims=True)
    flat_ids = expert_ids.reshape(-1)
    pair_count = flat_ids.shape[0]
    onehot = (flat_ids[:, None] == catalog).astype(jnp.bfloat16)
    pair_iota = jnp.arange(pair_count, dtype=jnp.int32)
    earlier = (pair_iota[None, :] < pair_iota[:, None]).astype(jnp.bfloat16)
    before = jnp.dot(earlier, onehot, preferred_element_type=jnp.float32)
    slot_index = jnp.sum(before * onehot.astype(jnp.float32), axis=1).astype(jnp.int32)
    dest_index = flat_ids * CAP + slot_index
    slot_total = expert_total * CAP
    slots = jnp.arange(slot_total, dtype=jnp.int32)
    dest_tok = dest_index.reshape(tok_rows, top_count)
    select_tok = jnp.any(dest_tok[None, :, :] == slots[:, None, None], axis=2).astype(jnp.bfloat16)
    local_experts = expert_total // col_count
    own_half = lax.dynamic_slice_in_dim(normed, core_index * half_width, half_width, axis=1)
    outgoing = jnp.dot(select_tok, own_half, preferred_element_type=jnp.float32)
    outgoing = outgoing.astype(jnp.bfloat16).reshape(col_count, local_experts, CAP, half_width)
    incoming_own = lax.all_to_all(outgoing, COL, split_axis=0, concat_axis=0, tiled=True)
    incoming_other = lax.ppermute(incoming_own, "core", perm=[(0, 1), (1, 0)])
    weights_own = lax.dynamic_slice_in_dim(expert_in, core_index * half_width, half_width, axis=2)
    weights_other = lax.dynamic_slice_in_dim(
        expert_in, (1 - core_index) * half_width, half_width, axis=2
    )
    gate_up = jnp.einsum(
        "secd,egdf->gsecf", incoming_own, weights_own, preferred_element_type=jnp.float32
    ) + jnp.einsum(
        "secd,egdf->gsecf", incoming_other, weights_other, preferred_element_type=jnp.float32
    )
    hidden = (jax.nn.silu(gate_up[0]) * gate_up[1]).astype(jnp.bfloat16)
    partial_out = jnp.einsum(
        "secf,efd->secd", hidden, row_order(expert_out, 2), preferred_element_type=jnp.float32
    )
    chip_sum = swap_reduce(partial_out.astype(jnp.bfloat16), "core", core_index, 3)
    send = chip_sum.astype(jnp.bfloat16).reshape(col_count, local_experts, CAP, 2, slice_width)
    send = send.transpose(3, 0, 1, 2, 4).reshape(2 * col_count, local_experts, CAP, slice_width)
    both = lax.all_to_all(send, ("xl",) + COL, split_axis=0, concat_axis=0, tiled=True)
    both = both.astype(jnp.float32).reshape(2, slot_total, slice_width)
    returned = (both[0] + both[1]).astype(jnp.bfloat16)
    pick = (dest_index[:, None] == slots[None, :]).astype(jnp.bfloat16)
    routed = jnp.dot(pick, returned, preferred_element_type=jnp.float32)
    routed = routed.reshape(tok_rows, top_count, slice_width)
    routed_sum = jnp.sum(gate_weights[:, :, None] * routed, axis=1)
    rows_each = shared_in.shape[1]
    stacked = jnp.concatenate(
        [shared_in.transpose(1, 0, 2), shared_out.T[:, None, :]], axis=1
    )
    sizes = {name: lax.axis_size(name) for name in COL}
    ring = ring_gather(stacked, "z", sizes["z"])
    ring = ring_gather(ring, "xh", sizes["xh"])
    ring = ring_gather(ring, "y", sizes["y"])
    ring = ring.reshape(col_count, rows_each, 3, ring.shape[-1])
    offsets = jnp.arange(col_count, dtype=jnp.int32)
    d_y = offsets // (sizes["xh"] * sizes["z"])
    d_xh = (offsets // sizes["z"]) % sizes["xh"]
    d_z = offsets % sizes["z"]
    me_y = lax.axis_index("y")
    me_xh = lax.axis_index("xh")
    me_z = lax.axis_index("z")
    source_col = (
        ((me_y - d_y) % sizes["y"]) * (sizes["xh"] * sizes["z"])
        + ((me_xh - d_xh) % sizes["xh"]) * sizes["z"]
        + (me_z - d_z) % sizes["z"]
    )
    normed_ring = jnp.take(normed.reshape(tok_rows, col_count, rows_each), source_col, axis=1)
    shared_acc = jnp.einsum(
        "tcj,cjgs->gts", normed_ring, ring[:, :, 0:2, :], preferred_element_type=jnp.float32
    )
    shared_hidden = (jax.nn.silu(shared_acc[0]) * shared_acc[1]).astype(jnp.bfloat16)
    terms_ring = jnp.einsum(
        "ts,cjs->tcj", shared_hidden, ring[:, :, 2, :], preferred_element_type=jnp.float32
    )
    cols = jnp.arange(col_count, dtype=jnp.int32)
    c_y = cols // (sizes["xh"] * sizes["z"])
    c_xh = (cols // sizes["z"]) % sizes["xh"]
    c_z = cols % sizes["z"]
    ring_of_col = (
        ((me_y - c_y) % sizes["y"]) * (sizes["xh"] * sizes["z"])
        + ((me_xh - c_xh) % sizes["xh"]) * sizes["z"]
        + (me_z - c_z) % sizes["z"]
    )
    shared_terms = jnp.take(terms_ring, ring_of_col, axis=1).reshape(tok_rows, width)
    shared_terms = row_order(shared_terms, 1)
    shared_half = swap_reduce(shared_terms.astype(jnp.bfloat16), "core", core_index, 1)
    shared_part = swap_reduce(shared_half.astype(jnp.bfloat16), "xl", xl_index, 1)
    mixed_out = (shared_part + routed_sum).astype(jnp.bfloat16)
    layers = kv_cache.shape[0]
    pairs = kv_cache.shape[1]
    requests = kv_cache.shape[2]
    slab_len = kv_cache.shape[4]
    head_slice = kv_cache.shape[5]
    piece_len = slab_len // (row_count * col_count)
    device_total = row_count * col_count
    span_local = jnp.einsum(
        "td,dph->tph", normed, kv_proj, preferred_element_type=jnp.float32
    ).astype(jnp.bfloat16)
    first_pos = CTX - tok_rows * col_count
    send_offset = (first_pos + col_index * tok_rows) % slab_len
    outbound = lax.dynamic_update_slice(
        jnp.zeros((slab_len, pairs, head_slice), jnp.bfloat16), span_local, (send_offset, 0, 0)
    )
    outbound = outbound.reshape(device_total, piece_len, pairs, head_slice)
    inbound = lax.all_to_all(outbound, AXES, split_axis=0, concat_axis=0, tiled=True)
    inbound = inbound.reshape(row_count, col_count, piece_len, pairs, head_slice)
    device_flat = row_index * col_count + col_index
    source_block = jnp.arange(col_count, dtype=jnp.int32)[:, None]
    within = device_flat * piece_len + jnp.arange(piece_len, dtype=jnp.int32)[None, :]
    offset_tok = (within - first_pos - source_block * tok_rows) % slab_len
    usable = offset_tok < tok_rows
    slab_of = (first_pos + source_block * tok_rows + offset_tok) // slab_len
    slab_ids = jnp.arange(col_count, dtype=jnp.int32)[:, None, None]
    placing = ((slab_of[None, :, :] == slab_ids) & usable[None, :, :]).astype(jnp.bfloat16)
    placed = jnp.einsum("sck,rckph->pskrh", placing, inbound, preferred_element_type=jnp.float32)
    placed = placed.reshape(pairs, col_count, piece_len, row_count * head_slice).astype(
        jnp.bfloat16
    )
    covered = jnp.sum(placing.astype(jnp.float32), axis=1) > 0.5
    first_long = jnp.min(jnp.where(lengths == CTX, jnp.arange(requests, dtype=jnp.int32), requests))
    relaid = relay_slabs(kv_cache, row_count, col_count)
    start_pos = (row_index * col_count + col_index) * piece_len
    places = (
        jnp.arange(col_count, dtype=jnp.int32)[:, None] * slab_len
        + start_pos
        + jnp.arange(piece_len, dtype=jnp.int32)[None, :]
    )
    live_mask = places[None, :, :] < lengths[:, None, None]
    cache_out = jnp.where(live_mask[None, None, :, :, :, None], relaid, jnp.zeros((), relaid.dtype))
    layer_pick = (jnp.arange(layers, dtype=jnp.int32) == layers - 1)[
        :, None, None, None, None, None
    ]
    request_pick = (jnp.arange(requests, dtype=jnp.int32) == first_long)[
        None, None, :, None, None, None
    ]
    select = layer_pick & request_pick & covered[None, None, None, :, :, None]
    cache_out = jnp.where(select, placed[None, :, None], cache_out)
    return (mixed_out, cache_out)


def solution(mesh):
    row_count = mesh.shape["row"]
    col_count = mesh.shape["col"]
    fine = Mesh(mesh.devices.reshape(2, row_count // 2, 4, 2, col_count // 8), AXES)

    def body(*args):
        return local(*args, row_count, col_count)

    return jax.shard_map(
        body,
        mesh=fine,
        in_specs=(
            P(COL, ROW),
            P(),
            P(COL, None),
            P(COL, None, None, ROW),
            P(COL, ROW, None),
            P(None, COL, ROW),
            P(ROW, COL),
            P(None, None, None, COL, None, ROW),
            P(),
            P(None, None, ROW),
        ),
        out_specs=(P(COL, ROW), P(None, None, None, None, AXES, None)),
        check_vma=False,
    )
```

```python
import jax
import jax.numpy as jnp
from jax import lax
from jax.sharding import Mesh
from jax.sharding import PartitionSpec as P

CTX = 16384
CAP = 32
ROW = ("xl", "core")
COL = ("y", "xh", "z")
AXES = ROW + COL


def relay_slabs(chosen, row_count, col_count):
    layers = chosen.shape[0]
    pairs = chosen.shape[1]
    requests = chosen.shape[2]
    slab_len = chosen.shape[4]
    head_width = chosen.shape[5]
    groups = layers * pairs * requests
    sectioned = chosen.reshape(groups, 1, slab_len, head_width)
    piece_len = slab_len // (row_count * col_count)
    relaid = lax.all_to_all(sectioned, AXES, split_axis=2, concat_axis=1, tiled=True)
    relaid = relaid.reshape(groups, row_count, col_count, piece_len, head_width)
    relaid = relaid.transpose(0, 2, 3, 1, 4).reshape(
        groups, col_count, piece_len, row_count * head_width
    )
    return relaid.reshape(layers, pairs, requests, col_count, piece_len, row_count * head_width)


def row_order(x, dim):
    shape = x.shape
    quarter = shape[dim] // 4
    split = x.reshape(shape[:dim] + (2, 2, quarter) + shape[dim + 1 :])
    return jnp.swapaxes(split, dim, dim + 1).reshape(shape)


def swap_gather(x, name, index):
    other = lax.ppermute(x, name, perm=[(0, 1), (1, 0)])
    return jnp.where(
        index == 0, jnp.concatenate([x, other], axis=-1), jnp.concatenate([other, x], axis=-1)
    )


def swap_reduce(x, name, index, dim):
    block = x.shape[dim] // 2
    keep = lax.dynamic_slice_in_dim(x, index * block, block, axis=dim)
    give = lax.dynamic_slice_in_dim(x, (1 - index) * block, block, axis=dim)
    got = lax.ppermute(give, name, perm=[(0, 1), (1, 0)])
    return keep.astype(jnp.float32) + got.astype(jnp.float32)


def local(
    tokens,
    router,
    expert_ids,
    expert_in,
    expert_out,
    shared_in,
    shared_out,
    kv_cache,
    lengths,
    kv_proj,
    row_count,
    col_count,
):
    row_index = lax.axis_index(ROW)
    col_index = lax.axis_index(COL)
    core_index = lax.axis_index("core")
    tok_rows = tokens.shape[0]
    slice_width = tokens.shape[1]
    xl_index = lax.axis_index("xl")
    gathered = swap_gather(tokens, "core", core_index)
    gathered = swap_gather(gathered, "xl", xl_index)
    width = gathered.shape[1]
    half_width = width // 2
    tokens_f = gathered.astype(jnp.float32)
    normed = (
        tokens_f * lax.rsqrt(jnp.mean(tokens_f * tokens_f, axis=-1, keepdims=True) + 1e-06)
    ).astype(jnp.bfloat16)
    logits = jnp.dot(normed, router, preferred_element_type=jnp.float32)
    expert_total = router.shape[1]
    top_count = expert_ids.shape[1]
    catalog = jnp.arange(expert_total, dtype=jnp.int32)
    matches = expert_ids[:, :, None] == catalog
    picked = jnp.sum(jnp.where(matches, logits[:, None, :], 0.0), axis=2)
    sigmoids = jax.nn.sigmoid(picked)
    gate_weights = sigmoids / jnp.sum(sigmoids, axis=1, keepdims=True)
    flat_ids = expert_ids.reshape(-1)
    pair_count = flat_ids.shape[0]
    onehot = (flat_ids[:, None] == catalog).astype(jnp.bfloat16)
    pair_iota = jnp.arange(pair_count, dtype=jnp.int32)
    earlier = (pair_iota[None, :] < pair_iota[:, None]).astype(jnp.bfloat16)
    before = jnp.dot(earlier, onehot, preferred_element_type=jnp.float32)
    slot_index = jnp.sum(before * onehot.astype(jnp.float32), axis=1).astype(jnp.int32)
    dest_index = flat_ids * CAP + slot_index
    slot_total = expert_total * CAP
    slots = jnp.arange(slot_total, dtype=jnp.int32)
    dest_tok = dest_index.reshape(tok_rows, top_count)
    select_tok = jnp.any(dest_tok[None, :, :] == slots[:, None, None], axis=2).astype(jnp.bfloat16)
    local_experts = expert_total // col_count
    own_half = lax.dynamic_slice_in_dim(normed, core_index * half_width, half_width, axis=1)
    outgoing = jnp.dot(select_tok, own_half, preferred_element_type=jnp.float32)
    outgoing = outgoing.astype(jnp.bfloat16).reshape(col_count, local_experts, CAP, half_width)
    incoming_own = lax.all_to_all(outgoing, COL, split_axis=0, concat_axis=0, tiled=True)
    incoming_other = lax.ppermute(incoming_own, "core", perm=[(0, 1), (1, 0)])
    weights_own = lax.dynamic_slice_in_dim(expert_in, core_index * half_width, half_width, axis=2)
    weights_other = lax.dynamic_slice_in_dim(
        expert_in, (1 - core_index) * half_width, half_width, axis=2
    )
    gate_up = jnp.einsum(
        "secd,egdf->gsecf", incoming_own, weights_own, preferred_element_type=jnp.float32
    ) + jnp.einsum(
        "secd,egdf->gsecf", incoming_other, weights_other, preferred_element_type=jnp.float32
    )
    hidden = (jax.nn.silu(gate_up[0]) * gate_up[1]).astype(jnp.bfloat16)
    partial_out = jnp.einsum(
        "secf,efd->secd", hidden, row_order(expert_out, 2), preferred_element_type=jnp.float32
    )
    chip_sum = swap_reduce(partial_out.astype(jnp.bfloat16), "core", core_index, 3)
    send = chip_sum.astype(jnp.bfloat16).reshape(col_count, local_experts, CAP, 2, slice_width)
    send = send.transpose(3, 0, 1, 2, 4).reshape(2 * col_count, local_experts, CAP, slice_width)
    both = lax.all_to_all(send, ("xl",) + COL, split_axis=0, concat_axis=0, tiled=True)
    both = both.astype(jnp.float32).reshape(2, slot_total, slice_width)
    returned = (both[0] + both[1]).astype(jnp.bfloat16)
    pick = (dest_index[:, None] == slots[None, :]).astype(jnp.bfloat16)
    routed = jnp.dot(pick, returned, preferred_element_type=jnp.float32)
    routed = routed.reshape(tok_rows, top_count, slice_width)
    routed_sum = jnp.sum(gate_weights[:, :, None] * routed, axis=1)
    stacked = jnp.concatenate(
        [shared_in.transpose(1, 0, 2), shared_out.T[:, None, :]], axis=1
    )
    shared_full = lax.all_gather(stacked, COL, axis=0, tiled=True)
    shared_acc = jnp.einsum(
        "td,dgs->gts", normed, shared_full[:, 0:2, :], preferred_element_type=jnp.float32
    )
    shared_hidden = (jax.nn.silu(shared_acc[0]) * shared_acc[1]).astype(jnp.bfloat16)
    shared_terms = jnp.einsum(
        "ts,ds->td", shared_hidden, shared_full[:, 2, :], preferred_element_type=jnp.float32
    )
    shared_terms = row_order(shared_terms, 1)
    shared_half = swap_reduce(shared_terms.astype(jnp.bfloat16), "core", core_index, 1)
    shared_part = swap_reduce(shared_half.astype(jnp.bfloat16), "xl", xl_index, 1)
    mixed_out = (shared_part + routed_sum).astype(jnp.bfloat16)
    layers = kv_cache.shape[0]
    pairs = kv_cache.shape[1]
    requests = kv_cache.shape[2]
    slab_len = kv_cache.shape[4]
    head_slice = kv_cache.shape[5]
    piece_len = slab_len // (row_count * col_count)
    device_total = row_count * col_count
    span_local = jnp.einsum(
        "td,dph->tph", normed, kv_proj, preferred_element_type=jnp.float32
    ).astype(jnp.bfloat16)
    first_pos = CTX - tok_rows * col_count
    send_offset = (first_pos + col_index * tok_rows) % slab_len
    outbound = lax.dynamic_update_slice(
        jnp.zeros((slab_len, pairs, head_slice), jnp.bfloat16), span_local, (send_offset, 0, 0)
    )
    outbound = outbound.reshape(device_total, piece_len, pairs, head_slice)
    inbound = lax.all_to_all(outbound, AXES, split_axis=0, concat_axis=0, tiled=True)
    inbound = inbound.reshape(row_count, col_count, piece_len, pairs, head_slice)
    device_flat = row_index * col_count + col_index
    source_block = jnp.arange(col_count, dtype=jnp.int32)[:, None]
    within = device_flat * piece_len + jnp.arange(piece_len, dtype=jnp.int32)[None, :]
    offset_tok = (within - first_pos - source_block * tok_rows) % slab_len
    usable = offset_tok < tok_rows
    slab_of = (first_pos + source_block * tok_rows + offset_tok) // slab_len
    slab_ids = jnp.arange(col_count, dtype=jnp.int32)[:, None, None]
    placing = ((slab_of[None, :, :] == slab_ids) & usable[None, :, :]).astype(jnp.bfloat16)
    placed = jnp.einsum("sck,rckph->pskrh", placing, inbound, preferred_element_type=jnp.float32)
    placed = placed.reshape(pairs, col_count, piece_len, row_count * head_slice).astype(
        jnp.bfloat16
    )
    covered = jnp.sum(placing.astype(jnp.float32), axis=1) > 0.5
    first_long = jnp.min(jnp.where(lengths == CTX, jnp.arange(requests, dtype=jnp.int32), requests))
    relaid = relay_slabs(kv_cache, row_count, col_count)
    start_pos = (row_index * col_count + col_index) * piece_len
    places = (
        jnp.arange(col_count, dtype=jnp.int32)[:, None] * slab_len
        + start_pos
        + jnp.arange(piece_len, dtype=jnp.int32)[None, :]
    )
    live_mask = places[None, :, :] < lengths[:, None, None]
    cache_out = jnp.where(live_mask[None, None, :, :, :, None], relaid, jnp.zeros((), relaid.dtype))
    layer_pick = (jnp.arange(layers, dtype=jnp.int32) == layers - 1)[
        :, None, None, None, None, None
    ]
    request_pick = (jnp.arange(requests, dtype=jnp.int32) == first_long)[
        None, None, :, None, None, None
    ]
    select = layer_pick & request_pick & covered[None, None, None, :, :, None]
    cache_out = jnp.where(select, placed[None, :, None], cache_out)
    return (mixed_out, cache_out)


def solution(mesh):
    row_count = mesh.shape["row"]
    col_count = mesh.shape["col"]
    fine = Mesh(mesh.devices.reshape(2, row_count // 2, 4, 2, col_count // 8), AXES)

    def body(*args):
        return local(*args, row_count, col_count)

    return jax.shard_map(
        body,
        mesh=fine,
        in_specs=(
            P(COL, ROW),
            P(),
            P(COL, None),
            P(COL, None, None, ROW),
            P(COL, ROW, None),
            P(None, COL, ROW),
            P(ROW, COL),
            P(None, None, None, COL, None, ROW),
            P(),
            P(None, None, ROW),
        ),
        out_specs=(P(COL, ROW), P(None, None, None, None, AXES, None)),
        check_vma=False,
    )
```

```python
import jax
import jax.numpy as jnp
from jax import lax
from jax.sharding import Mesh
from jax.sharding import PartitionSpec as P

CTX = 16384
CAP = 32
ROW = ("xl", "core")
COL = ("y", "xh", "z")
AXES = ROW + COL


def relay_slabs(chosen, row_count, col_count):
    layers = chosen.shape[0]
    pairs = chosen.shape[1]
    requests = chosen.shape[2]
    slab_len = chosen.shape[4]
    head_width = chosen.shape[5]
    groups = layers * pairs * requests
    sectioned = chosen.reshape(groups, 1, slab_len, head_width)
    piece_len = slab_len // (row_count * col_count)
    relaid = lax.all_to_all(sectioned, AXES, split_axis=2, concat_axis=1, tiled=True)
    relaid = relaid.reshape(groups, row_count, col_count, piece_len, head_width)
    relaid = relaid.transpose(0, 2, 3, 1, 4).reshape(
        groups, col_count, piece_len, row_count * head_width
    )
    return relaid.reshape(layers, pairs, requests, col_count, piece_len, row_count * head_width)


def row_order(x, dim):
    shape = x.shape
    quarter = shape[dim] // 4
    split = x.reshape(shape[:dim] + (2, 2, quarter) + shape[dim + 1 :])
    return jnp.swapaxes(split, dim, dim + 1).reshape(shape)


def swap_gather(x, name, index):
    other = lax.ppermute(x, name, perm=[(0, 1), (1, 0)])
    return jnp.where(
        index == 0, jnp.concatenate([x, other], axis=-1), jnp.concatenate([other, x], axis=-1)
    )


def swap_reduce(x, name, index, dim):
    block = x.shape[dim] // 2
    keep = lax.dynamic_slice_in_dim(x, index * block, block, axis=dim)
    give = lax.dynamic_slice_in_dim(x, (1 - index) * block, block, axis=dim)
    got = lax.ppermute(give, name, perm=[(0, 1), (1, 0)])
    return keep.astype(jnp.float32) + got.astype(jnp.float32)


def local(
    tokens,
    router,
    expert_ids,
    expert_in,
    expert_out,
    shared_in,
    shared_out,
    kv_cache,
    lengths,
    kv_proj,
    row_count,
    col_count,
):
    row_index = lax.axis_index(ROW)
    col_index = lax.axis_index(COL)
    core_index = lax.axis_index("core")
    tok_rows = tokens.shape[0]
    slice_width = tokens.shape[1]
    xl_index = lax.axis_index("xl")
    gathered = swap_gather(tokens, "core", core_index)
    gathered = swap_gather(gathered, "xl", xl_index)
    width = gathered.shape[1]
    half_width = width // 2
    tokens_f = gathered.astype(jnp.float32)
    normed = (
        tokens_f * lax.rsqrt(jnp.mean(tokens_f * tokens_f, axis=-1, keepdims=True) + 1e-06)
    ).astype(jnp.bfloat16)
    logits = jnp.dot(normed, router, preferred_element_type=jnp.float32)
    expert_total = router.shape[1]
    top_count = expert_ids.shape[1]
    catalog = jnp.arange(expert_total, dtype=jnp.int32)
    matches = expert_ids[:, :, None] == catalog
    picked = jnp.sum(jnp.where(matches, logits[:, None, :], 0.0), axis=2)
    sigmoids = jax.nn.sigmoid(picked)
    gate_weights = sigmoids / jnp.sum(sigmoids, axis=1, keepdims=True)
    flat_ids = expert_ids.reshape(-1)
    pair_count = flat_ids.shape[0]
    onehot = (flat_ids[:, None] == catalog).astype(jnp.bfloat16)
    pair_iota = jnp.arange(pair_count, dtype=jnp.int32)
    earlier = (pair_iota[None, :] < pair_iota[:, None]).astype(jnp.bfloat16)
    before = jnp.dot(earlier, onehot, preferred_element_type=jnp.float32)
    slot_index = jnp.sum(before * onehot.astype(jnp.float32), axis=1).astype(jnp.int32)
    dest_index = flat_ids * CAP + slot_index
    slot_total = expert_total * CAP
    slots = jnp.arange(slot_total, dtype=jnp.int32)
    dest_tok = dest_index.reshape(tok_rows, top_count)
    select_tok = jnp.any(dest_tok[None, :, :] == slots[:, None, None], axis=2).astype(jnp.bfloat16)
    local_experts = expert_total // col_count
    own_half = lax.dynamic_slice_in_dim(normed, core_index * half_width, half_width, axis=1)
    outgoing = jnp.dot(select_tok, own_half, preferred_element_type=jnp.float32)
    outgoing = outgoing.astype(jnp.bfloat16).reshape(col_count, local_experts, CAP, half_width)
    incoming_own = lax.all_to_all(outgoing, COL, split_axis=0, concat_axis=1, tiled=False)
    incoming_other = lax.ppermute(incoming_own, "core", perm=[(0, 1), (1, 0)])
    weights_own = lax.dynamic_slice_in_dim(expert_in, core_index * half_width, half_width, axis=2)
    weights_other = lax.dynamic_slice_in_dim(
        expert_in, (1 - core_index) * half_width, half_width, axis=2
    )
    gate_up = jnp.einsum(
        "escd,egdf->gescf", incoming_own, weights_own, preferred_element_type=jnp.float32
    ) + jnp.einsum(
        "escd,egdf->gescf", incoming_other, weights_other, preferred_element_type=jnp.float32
    )
    hidden = (jax.nn.silu(gate_up[0]) * gate_up[1]).astype(jnp.bfloat16)
    quarter_parts = [
        jnp.einsum(
            "escf,efd->secd",
            hidden,
            expert_out[:, :, q * slice_width : (q + 1) * slice_width],
            preferred_element_type=jnp.float32,
        ).astype(jnp.bfloat16)
        for q in range(4)
    ]
    on_first = core_index == 0
    keep = jnp.stack(
        [
            jnp.where(on_first, quarter_parts[0], quarter_parts[1]),
            jnp.where(on_first, quarter_parts[2], quarter_parts[3]),
        ]
    )
    give = jnp.stack(
        [
            jnp.where(on_first, quarter_parts[1], quarter_parts[0]),
            jnp.where(on_first, quarter_parts[3], quarter_parts[2]),
        ]
    )
    got = lax.ppermute(give, "core", perm=[(0, 1), (1, 0)])
    chip_sum = (keep.astype(jnp.float32) + got.astype(jnp.float32)).astype(jnp.bfloat16)
    send = chip_sum.reshape(2 * col_count, local_experts * CAP, slice_width)
    both = lax.all_to_all(send, ("xl",) + COL, split_axis=0, concat_axis=0, tiled=True)
    both = both.astype(jnp.float32).reshape(2, slot_total, slice_width)
    returned = (both[0] + both[1]).astype(jnp.bfloat16)
    pick = (dest_index[:, None] == slots[None, :]).astype(jnp.bfloat16)
    routed = jnp.dot(pick, returned, preferred_element_type=jnp.float32)
    routed = routed.reshape(tok_rows, top_count, slice_width)
    routed_sum = jnp.sum(gate_weights[:, :, None] * routed, axis=1)
    stacked = jnp.concatenate(
        [shared_in.transpose(1, 0, 2), shared_out.T[:, None, :]], axis=1
    )
    shared_full = lax.all_gather(stacked, COL, axis=0, tiled=True)
    shared_acc = jnp.einsum(
        "td,dgs->gts", normed, shared_full[:, 0:2, :], preferred_element_type=jnp.float32
    )
    shared_hidden = (jax.nn.silu(shared_acc[0]) * shared_acc[1]).astype(jnp.bfloat16)
    shared_terms = jnp.einsum(
        "ts,ds->td", shared_hidden, shared_full[:, 2, :], preferred_element_type=jnp.float32
    )
    shared_terms = row_order(shared_terms, 1)
    shared_half = swap_reduce(shared_terms.astype(jnp.bfloat16), "core", core_index, 1)
    shared_part = swap_reduce(shared_half.astype(jnp.bfloat16), "xl", xl_index, 1)
    mixed_out = (shared_part + routed_sum).astype(jnp.bfloat16)
    layers = kv_cache.shape[0]
    pairs = kv_cache.shape[1]
    requests = kv_cache.shape[2]
    slab_len = kv_cache.shape[4]
    head_slice = kv_cache.shape[5]
    piece_len = slab_len // (row_count * col_count)
    device_total = row_count * col_count
    span_local = jnp.einsum(
        "td,dph->tph", normed, kv_proj, preferred_element_type=jnp.float32
    ).astype(jnp.bfloat16)
    first_pos = CTX - tok_rows * col_count
    send_offset = (first_pos + col_index * tok_rows) % slab_len
    outbound = lax.dynamic_update_slice(
        jnp.zeros((slab_len, pairs, head_slice), jnp.bfloat16), span_local, (send_offset, 0, 0)
    )
    outbound = outbound.reshape(device_total, piece_len, pairs, head_slice)
    inbound = lax.all_to_all(outbound, AXES, split_axis=0, concat_axis=0, tiled=True)
    inbound = inbound.reshape(row_count, col_count, piece_len, pairs, head_slice)
    device_flat = row_index * col_count + col_index
    source_block = jnp.arange(col_count, dtype=jnp.int32)[:, None]
    within = device_flat * piece_len + jnp.arange(piece_len, dtype=jnp.int32)[None, :]
    offset_tok = (within - first_pos - source_block * tok_rows) % slab_len
    usable = offset_tok < tok_rows
    slab_of = (first_pos + source_block * tok_rows + offset_tok) // slab_len
    slab_ids = jnp.arange(col_count, dtype=jnp.int32)[:, None, None]
    placing = ((slab_of[None, :, :] == slab_ids) & usable[None, :, :]).astype(jnp.bfloat16)
    placed = jnp.einsum("sck,rckph->pskrh", placing, inbound, preferred_element_type=jnp.float32)
    placed = placed.reshape(pairs, col_count, piece_len, row_count * head_slice).astype(
        jnp.bfloat16
    )
    covered = jnp.sum(placing.astype(jnp.float32), axis=1) > 0.5
    first_long = jnp.min(jnp.where(lengths == CTX, jnp.arange(requests, dtype=jnp.int32), requests))
    relaid = relay_slabs(kv_cache, row_count, col_count)
    start_pos = (row_index * col_count + col_index) * piece_len
    places = (
        jnp.arange(col_count, dtype=jnp.int32)[:, None] * slab_len
        + start_pos
        + jnp.arange(piece_len, dtype=jnp.int32)[None, :]
    )
    live_mask = places[None, :, :] < lengths[:, None, None]
    cache_out = jnp.where(live_mask[None, None, :, :, :, None], relaid, jnp.zeros((), relaid.dtype))
    layer_pick = (jnp.arange(layers, dtype=jnp.int32) == layers - 1)[
        :, None, None, None, None, None
    ]
    request_pick = (jnp.arange(requests, dtype=jnp.int32) == first_long)[
        None, None, :, None, None, None
    ]
    select = layer_pick & request_pick & covered[None, None, None, :, :, None]
    cache_out = jnp.where(select, placed[None, :, None], cache_out)
    return (mixed_out, cache_out)


def solution(mesh):
    row_count = mesh.shape["row"]
    col_count = mesh.shape["col"]
    fine = Mesh(mesh.devices.reshape(2, row_count // 2, 4, 2, col_count // 8), AXES)

    def body(*args):
        return local(*args, row_count, col_count)

    return jax.shard_map(
        body,
        mesh=fine,
        in_specs=(
            P(COL, ROW),
            P(),
            P(COL, None),
            P(COL, None, None, ROW),
            P(COL, ROW, None),
            P(None, COL, ROW),
            P(ROW, COL),
            P(None, None, None, COL, None, ROW),
            P(),
            P(None, None, ROW),
        ),
        out_specs=(P(COL, ROW), P(None, None, None, None, AXES, None)),
        check_vma=False,
    )
```

```python
import jax
import jax.numpy as jnp
from jax import lax
from jax.sharding import Mesh
from jax.sharding import PartitionSpec as P

CTX = 16384
CAP = 32
SHORT = 256
ROW = ("xl", "core")
COL = ("y", "xh", "z")
AXES = ROW + COL


def row_order(x, dim):
    shape = x.shape
    quarter = shape[dim] // 4
    split = x.reshape(shape[:dim] + (2, 2, quarter) + shape[dim + 1 :])
    return jnp.swapaxes(split, dim, dim + 1).reshape(shape)


def swap_gather(x, name, index):
    other = lax.ppermute(x, name, perm=[(0, 1), (1, 0)])
    return jnp.where(
        index == 0, jnp.concatenate([x, other], axis=-1), jnp.concatenate([other, x], axis=-1)
    )


def swap_reduce(x, name, index, dim):
    block = x.shape[dim] // 2
    keep = lax.dynamic_slice_in_dim(x, index * block, block, axis=dim)
    give = lax.dynamic_slice_in_dim(x, (1 - index) * block, block, axis=dim)
    got = lax.ppermute(give, name, perm=[(0, 1), (1, 0)])
    return keep.astype(jnp.float32) + got.astype(jnp.float32)


def local(
    tokens,
    router,
    expert_ids,
    expert_in,
    expert_out,
    shared_in,
    shared_out,
    kv_cache,
    lengths,
    kv_proj,
    row_count,
    col_count,
):
    row_index = lax.axis_index(ROW)
    col_index = lax.axis_index(COL)
    core_index = lax.axis_index("core")
    tok_rows = tokens.shape[0]
    slice_width = tokens.shape[1]
    xl_index = lax.axis_index("xl")
    gathered = swap_gather(tokens, "core", core_index)
    gathered = swap_gather(gathered, "xl", xl_index)
    width = gathered.shape[1]
    half_width = width // 2
    tokens_f = gathered.astype(jnp.float32)
    normed = (
        tokens_f * lax.rsqrt(jnp.mean(tokens_f * tokens_f, axis=-1, keepdims=True) + 1e-06)
    ).astype(jnp.bfloat16)
    logits = jnp.dot(normed, router, preferred_element_type=jnp.float32)
    expert_total = router.shape[1]
    top_count = expert_ids.shape[1]
    catalog = jnp.arange(expert_total, dtype=jnp.int32)
    matches = expert_ids[:, :, None] == catalog
    picked = jnp.sum(jnp.where(matches, logits[:, None, :], 0.0), axis=2)
    sigmoids = jax.nn.sigmoid(picked)
    gate_weights = sigmoids / jnp.sum(sigmoids, axis=1, keepdims=True)
    flat_ids = expert_ids.reshape(-1)
    pair_count = flat_ids.shape[0]
    onehot = (flat_ids[:, None] == catalog).astype(jnp.bfloat16)
    pair_iota = jnp.arange(pair_count, dtype=jnp.int32)
    earlier = (pair_iota[None, :] < pair_iota[:, None]).astype(jnp.bfloat16)
    before = jnp.dot(earlier, onehot, preferred_element_type=jnp.float32)
    slot_index = jnp.sum(before * onehot.astype(jnp.float32), axis=1).astype(jnp.int32)
    dest_index = flat_ids * CAP + slot_index
    slot_total = expert_total * CAP
    slots = jnp.arange(slot_total, dtype=jnp.int32)
    dest_tok = dest_index.reshape(tok_rows, top_count)
    select_tok = jnp.any(dest_tok[None, :, :] == slots[:, None, None], axis=2).astype(jnp.bfloat16)
    local_experts = expert_total // col_count
    own_half = lax.dynamic_slice_in_dim(normed, core_index * half_width, half_width, axis=1)
    outgoing = jnp.dot(select_tok, own_half, preferred_element_type=jnp.float32)
    outgoing = outgoing.astype(jnp.bfloat16).reshape(col_count, local_experts, CAP, half_width)
    incoming_own = lax.all_to_all(outgoing, COL, split_axis=0, concat_axis=1, tiled=False)
    incoming_other = lax.ppermute(incoming_own, "core", perm=[(0, 1), (1, 0)])
    weights_own = lax.dynamic_slice_in_dim(expert_in, core_index * half_width, half_width, axis=2)
    weights_other = lax.dynamic_slice_in_dim(
        expert_in, (1 - core_index) * half_width, half_width, axis=2
    )
    gate_up = jnp.einsum(
        "escd,egdf->gescf", incoming_own, weights_own, preferred_element_type=jnp.float32
    ) + jnp.einsum(
        "escd,egdf->gescf", incoming_other, weights_other, preferred_element_type=jnp.float32
    )
    hidden = (jax.nn.silu(gate_up[0]) * gate_up[1]).astype(jnp.bfloat16)
    quarter_parts = [
        jnp.einsum(
            "escf,efd->secd",
            hidden,
            expert_out[:, :, q * slice_width : (q + 1) * slice_width],
            preferred_element_type=jnp.float32,
        ).astype(jnp.bfloat16)
        for q in range(4)
    ]
    on_first = core_index == 0
    keep = jnp.stack(
        [
            jnp.where(on_first, quarter_parts[0], quarter_parts[1]),
            jnp.where(on_first, quarter_parts[2], quarter_parts[3]),
        ]
    )
    give = jnp.stack(
        [
            jnp.where(on_first, quarter_parts[1], quarter_parts[0]),
            jnp.where(on_first, quarter_parts[3], quarter_parts[2]),
        ]
    )
    got = lax.ppermute(give, "core", perm=[(0, 1), (1, 0)])
    chip_sum = (keep.astype(jnp.float32) + got.astype(jnp.float32)).astype(jnp.bfloat16)
    send = chip_sum.reshape(2 * col_count, local_experts * CAP, slice_width)
    both = lax.all_to_all(send, ("xl",) + COL, split_axis=0, concat_axis=0, tiled=True)
    both = both.astype(jnp.float32).reshape(2, slot_total, slice_width)
    returned = (both[0] + both[1]).astype(jnp.bfloat16)
    pick = (dest_index[:, None] == slots[None, :]).astype(jnp.bfloat16)
    routed = jnp.dot(pick, returned, preferred_element_type=jnp.float32)
    routed = routed.reshape(tok_rows, top_count, slice_width)
    routed_sum = jnp.sum(gate_weights[:, :, None] * routed, axis=1)
    stacked = jnp.concatenate(
        [shared_in.transpose(1, 0, 2), shared_out.T[:, None, :]], axis=1
    )
    shared_full = lax.all_gather(stacked, COL, axis=0, tiled=True)
    shared_acc = jnp.einsum(
        "td,dgs->gts", normed, shared_full[:, 0:2, :], preferred_element_type=jnp.float32
    )
    shared_hidden = (jax.nn.silu(shared_acc[0]) * shared_acc[1]).astype(jnp.bfloat16)
    shared_terms = jnp.einsum(
        "ts,ds->td", shared_hidden, shared_full[:, 2, :], preferred_element_type=jnp.float32
    )
    shared_terms = row_order(shared_terms, 1)
    shared_half = swap_reduce(shared_terms.astype(jnp.bfloat16), "core", core_index, 1)
    shared_part = swap_reduce(shared_half.astype(jnp.bfloat16), "xl", xl_index, 1)
    mixed_out = (shared_part + routed_sum).astype(jnp.bfloat16)
    layers, pairs, requests, _, slab_len, head_slice = kv_cache.shape
    device_total = row_count * col_count
    piece_len = slab_len // device_total
    span_local = jnp.einsum(
        "td,dph->tph", normed, kv_proj, preferred_element_type=jnp.float32
    ).astype(jnp.bfloat16)
    first_pos = CTX - tok_rows * col_count
    blocks_per_slab = slab_len // tok_rows
    first_span_slab = first_pos // slab_len
    span_pih = span_local.transpose(1, 0, 2)
    span_parts = []
    for part in range(blocks_per_slab):
        perm = [
            (b, first_span_slab + b // blocks_per_slab)
            for b in range(col_count)
            if b % blocks_per_slab == part
        ]
        span_parts.append(lax.ppermute(span_pih, COL, perm=perm))
    span_slab = jnp.concatenate(span_parts, axis=1)
    request_ids = jnp.arange(requests, dtype=jnp.int32)
    long_id = jnp.min(jnp.where(lengths == CTX, request_ids, requests))
    short_id = requests - 1 - long_id
    slab_data = kv_cache[:, :, :, 0]
    long_local = lax.dynamic_index_in_dim(slab_data, long_id, axis=2, keepdims=False)
    short_local = lax.dynamic_index_in_dim(slab_data, short_id, axis=2, keepdims=False)
    last_layer = jnp.where(col_index >= first_span_slab, span_slab, long_local[layers - 1])
    payload = jnp.concatenate([long_local[: layers - 1], last_layer[None]], axis=0)
    payload = payload.reshape(layers * pairs, device_total, piece_len, head_slice)
    relaid = lax.all_to_all(payload, AXES, split_axis=1, concat_axis=0, tiled=False)
    long_out = relaid.reshape(row_count, col_count, layers, pairs, piece_len, head_slice)
    long_out = long_out.transpose(2, 3, 1, 4, 0, 5).reshape(
        layers, pairs, col_count, piece_len, row_count * head_slice
    )
    short_rows = SHORT // (col_count * piece_len)
    short_head = short_local[:, :, :SHORT].reshape(
        layers * pairs, short_rows, col_count, piece_len, head_slice
    )
    short_cols = lax.all_to_all(short_head, COL, split_axis=2, concat_axis=0, tiled=False)[0]
    short_cols = jnp.concatenate(
        [
            short_cols,
            jnp.zeros(
                (layers * pairs, row_count - short_rows, piece_len, head_slice), jnp.bfloat16
            ),
        ],
        axis=1,
    )
    short_piece = lax.all_to_all(short_cols, ROW, split_axis=1, concat_axis=0, tiled=False)
    short_piece = short_piece.transpose(1, 2, 0, 3).reshape(
        layers, pairs, piece_len, row_count * head_slice
    )
    positions = (row_index * col_count + col_index) * piece_len + jnp.arange(
        piece_len, dtype=jnp.int32
    )
    short_live = positions < lengths[short_id]
    slab_ids = jnp.arange(col_count, dtype=jnp.int32)
    short_keep = (slab_ids[:, None] == 0) & short_live[None, :]
    short_out = jnp.where(
        short_keep[None, None, :, :, None], short_piece[:, :, None], jnp.zeros((), jnp.bfloat16)
    )
    cache_out = jnp.where(
        (request_ids == long_id)[None, None, :, None, None, None],
        long_out[:, :, None],
        short_out[:, :, None],
    )
    return (mixed_out, cache_out)


def solution(mesh):
    row_count = mesh.shape["row"]
    col_count = mesh.shape["col"]
    fine = Mesh(mesh.devices.reshape(2, row_count // 2, 4, 2, col_count // 8), AXES)

    def body(*args):
        return local(*args, row_count, col_count)

    return jax.shard_map(
        body,
        mesh=fine,
        in_specs=(
            P(COL, ROW),
            P(),
            P(COL, None),
            P(COL, None, None, ROW),
            P(COL, ROW, None),
            P(None, COL, ROW),
            P(ROW, COL),
            P(None, None, None, COL, None, ROW),
            P(),
            P(None, None, ROW),
        ),
        out_specs=(P(COL, ROW), P(None, None, None, None, AXES, None)),
        check_vma=False,
    )
```

```python
import jax
import jax.numpy as jnp
from jax import lax
from jax.sharding import Mesh
from jax.sharding import PartitionSpec as P

CTX = 16384
CAP = 32
SHORT = 256
ROW = ("xl", "core")
COL = ("y", "xh", "z")
AXES = ROW + COL


def row_order(x, dim):
    shape = x.shape
    quarter = shape[dim] // 4
    split = x.reshape(shape[:dim] + (2, 2, quarter) + shape[dim + 1 :])
    return jnp.swapaxes(split, dim, dim + 1).reshape(shape)


def swap_gather(x, name, index):
    other = lax.ppermute(x, name, perm=[(0, 1), (1, 0)])
    return jnp.where(
        index == 0, jnp.concatenate([x, other], axis=-1), jnp.concatenate([other, x], axis=-1)
    )


def swap_reduce(x, name, index, dim):
    block = x.shape[dim] // 2
    keep = lax.dynamic_slice_in_dim(x, index * block, block, axis=dim)
    give = lax.dynamic_slice_in_dim(x, (1 - index) * block, block, axis=dim)
    got = lax.ppermute(give, name, perm=[(0, 1), (1, 0)])
    return keep.astype(jnp.float32) + got.astype(jnp.float32)


def local(
    tokens,
    router,
    expert_ids,
    expert_in,
    expert_out,
    shared_in,
    shared_out,
    kv_cache,
    lengths,
    kv_proj,
    row_count,
    col_count,
):
    row_index = lax.axis_index(ROW)
    col_index = lax.axis_index(COL)
    core_index = lax.axis_index("core")
    tok_rows = tokens.shape[0]
    slice_width = tokens.shape[1]
    xl_index = lax.axis_index("xl")
    gathered = swap_gather(tokens, "core", core_index)
    gathered = swap_gather(gathered, "xl", xl_index)
    width = gathered.shape[1]
    half_width = width // 2
    tokens_f = gathered.astype(jnp.float32)
    normed = (
        tokens_f * lax.rsqrt(jnp.mean(tokens_f * tokens_f, axis=-1, keepdims=True) + 1e-06)
    ).astype(jnp.bfloat16)
    logits = jnp.dot(normed, router, preferred_element_type=jnp.float32)
    expert_total = router.shape[1]
    top_count = expert_ids.shape[1]
    catalog = jnp.arange(expert_total, dtype=jnp.int32)
    matches = expert_ids[:, :, None] == catalog
    picked = jnp.sum(jnp.where(matches, logits[:, None, :], 0.0), axis=2)
    sigmoids = jax.nn.sigmoid(picked)
    gate_weights = sigmoids / jnp.sum(sigmoids, axis=1, keepdims=True)
    flat_ids = expert_ids.reshape(-1)
    pair_count = flat_ids.shape[0]
    onehot = (flat_ids[:, None] == catalog).astype(jnp.bfloat16)
    pair_iota = jnp.arange(pair_count, dtype=jnp.int32)
    earlier = (pair_iota[None, :] < pair_iota[:, None]).astype(jnp.bfloat16)
    before = jnp.dot(earlier, onehot, preferred_element_type=jnp.float32)
    slot_index = jnp.sum(before * onehot.astype(jnp.float32), axis=1).astype(jnp.int32)
    dest_index = flat_ids * CAP + slot_index
    slot_total = expert_total * CAP
    slots = jnp.arange(slot_total, dtype=jnp.int32)
    dest_tok = dest_index.reshape(tok_rows, top_count)
    select_tok = jnp.any(dest_tok[None, :, :] == slots[:, None, None], axis=2).astype(jnp.bfloat16)
    local_experts = expert_total // col_count
    own_half = lax.dynamic_slice_in_dim(normed, core_index * half_width, half_width, axis=1)
    outgoing = jnp.dot(select_tok, own_half, preferred_element_type=jnp.float32)
    outgoing = outgoing.astype(jnp.bfloat16).reshape(col_count, local_experts, CAP, half_width)
    incoming_own = lax.all_to_all(outgoing, COL, split_axis=0, concat_axis=1, tiled=False)
    incoming_other = lax.ppermute(incoming_own, "core", perm=[(0, 1), (1, 0)])
    weights_own = lax.dynamic_slice_in_dim(expert_in, core_index * half_width, half_width, axis=2)
    weights_other = lax.dynamic_slice_in_dim(
        expert_in, (1 - core_index) * half_width, half_width, axis=2
    )
    gate_up = jnp.einsum(
        "escd,egdf->gescf", incoming_own, weights_own, preferred_element_type=jnp.float32
    ) + jnp.einsum(
        "escd,egdf->gescf", incoming_other, weights_other, preferred_element_type=jnp.float32
    )
    hidden = (jax.nn.silu(gate_up[0]) * gate_up[1]).astype(jnp.bfloat16)
    quarter_parts = [
        jnp.einsum(
            "escf,efd->secd",
            hidden,
            expert_out[:, :, q * slice_width : (q + 1) * slice_width],
            preferred_element_type=jnp.float32,
        ).astype(jnp.bfloat16)
        for q in range(4)
    ]
    on_first = core_index == 0
    keep = jnp.stack(
        [
            jnp.where(on_first, quarter_parts[0], quarter_parts[1]),
            jnp.where(on_first, quarter_parts[2], quarter_parts[3]),
        ]
    )
    give = jnp.stack(
        [
            jnp.where(on_first, quarter_parts[1], quarter_parts[0]),
            jnp.where(on_first, quarter_parts[3], quarter_parts[2]),
        ]
    )
    got = lax.ppermute(give, "core", perm=[(0, 1), (1, 0)])
    chip_sum = (keep.astype(jnp.float32) + got.astype(jnp.float32)).astype(jnp.bfloat16)
    send = chip_sum.reshape(2 * col_count, local_experts * CAP, slice_width)
    layers, pairs, requests, _, slab_len, head_slice = kv_cache.shape
    device_total = row_count * col_count
    piece_len = slab_len // device_total
    span_local = jnp.einsum(
        "td,dph->tph", normed, kv_proj, preferred_element_type=jnp.float32
    ).astype(jnp.bfloat16)
    first_pos = CTX - tok_rows * col_count
    blocks_per_slab = slab_len // tok_rows
    first_span_slab = first_pos // slab_len
    span_pih = span_local.transpose(1, 0, 2)
    span_parts = []
    for part in range(blocks_per_slab):
        perm = [
            (b, first_span_slab + b // blocks_per_slab)
            for b in range(col_count)
            if b % blocks_per_slab == part
        ]
        span_parts.append(lax.ppermute(span_pih, COL, perm=perm))
    span_slab = jnp.concatenate(span_parts, axis=1)
    request_ids = jnp.arange(requests, dtype=jnp.int32)
    long_id = jnp.min(jnp.where(lengths == CTX, request_ids, requests))
    short_id = requests - 1 - long_id
    slab_data = kv_cache[:, :, :, 0]
    long_local = lax.dynamic_index_in_dim(slab_data, long_id, axis=2, keepdims=False)
    short_local = lax.dynamic_index_in_dim(slab_data, short_id, axis=2, keepdims=False)
    last_layer = jnp.where(col_index >= first_span_slab, span_slab, long_local[layers - 1])
    payload = jnp.concatenate([long_local[: layers - 1], last_layer[None]], axis=0)
    payload = payload.reshape(layers * pairs, device_total, piece_len, head_slice)
    both = lax.all_to_all(send, ("xl",) + COL, split_axis=0, concat_axis=0, tiled=True)
    both, payload, short_local = lax.optimization_barrier((both, payload, short_local))
    both = both.astype(jnp.float32).reshape(2, slot_total, slice_width)
    returned = (both[0] + both[1]).astype(jnp.bfloat16)
    pick = (dest_index[:, None] == slots[None, :]).astype(jnp.bfloat16)
    routed = jnp.dot(pick, returned, preferred_element_type=jnp.float32)
    routed = routed.reshape(tok_rows, top_count, slice_width)
    routed_sum = jnp.sum(gate_weights[:, :, None] * routed, axis=1)
    stacked = jnp.concatenate(
        [shared_in.transpose(1, 0, 2), shared_out.T[:, None, :]], axis=1
    )
    shared_full = lax.all_gather(stacked, COL, axis=0, tiled=True)
    shared_acc = jnp.einsum(
        "td,dgs->gts", normed, shared_full[:, 0:2, :], preferred_element_type=jnp.float32
    )
    shared_hidden = (jax.nn.silu(shared_acc[0]) * shared_acc[1]).astype(jnp.bfloat16)
    shared_terms = jnp.einsum(
        "ts,ds->td", shared_hidden, shared_full[:, 2, :], preferred_element_type=jnp.float32
    )
    shared_terms = row_order(shared_terms, 1)
    shared_half = swap_reduce(shared_terms.astype(jnp.bfloat16), "core", core_index, 1)
    shared_part = swap_reduce(shared_half.astype(jnp.bfloat16), "xl", xl_index, 1)
    mixed_out = (shared_part + routed_sum).astype(jnp.bfloat16)
    relaid = lax.all_to_all(payload, AXES, split_axis=1, concat_axis=0, tiled=False)
    long_out = relaid.reshape(row_count, col_count, layers, pairs, piece_len, head_slice)
    long_out = long_out.transpose(2, 3, 1, 4, 0, 5).reshape(
        layers, pairs, col_count, piece_len, row_count * head_slice
    )
    short_rows = SHORT // (col_count * piece_len)
    short_head = short_local[:, :, :SHORT].reshape(
        layers * pairs, short_rows, col_count, piece_len, head_slice
    )
    short_cols = lax.all_to_all(short_head, COL, split_axis=2, concat_axis=0, tiled=False)[0]
    short_cols = jnp.concatenate(
        [
            short_cols,
            jnp.zeros(
                (layers * pairs, row_count - short_rows, piece_len, head_slice), jnp.bfloat16
            ),
        ],
        axis=1,
    )
    short_piece = lax.all_to_all(short_cols, ROW, split_axis=1, concat_axis=0, tiled=False)
    short_piece = short_piece.transpose(1, 2, 0, 3).reshape(
        layers, pairs, piece_len, row_count * head_slice
    )
    positions = (row_index * col_count + col_index) * piece_len + jnp.arange(
        piece_len, dtype=jnp.int32
    )
    short_live = positions < lengths[short_id]
    slab_ids = jnp.arange(col_count, dtype=jnp.int32)
    short_keep = (slab_ids[:, None] == 0) & short_live[None, :]
    short_out = jnp.where(
        short_keep[None, None, :, :, None], short_piece[:, :, None], jnp.zeros((), jnp.bfloat16)
    )
    cache_out = jnp.where(
        (request_ids == long_id)[None, None, :, None, None, None],
        long_out[:, :, None],
        short_out[:, :, None],
    )
    return (mixed_out, cache_out)


def solution(mesh):
    row_count = mesh.shape["row"]
    col_count = mesh.shape["col"]
    fine = Mesh(mesh.devices.reshape(2, row_count // 2, 4, 2, col_count // 8), AXES)

    def body(*args):
        return local(*args, row_count, col_count)

    return jax.shard_map(
        body,
        mesh=fine,
        in_specs=(
            P(COL, ROW),
            P(),
            P(COL, None),
            P(COL, None, None, ROW),
            P(COL, ROW, None),
            P(None, COL, ROW),
            P(ROW, COL),
            P(None, None, None, COL, None, ROW),
            P(),
            P(None, None, ROW),
        ),
        out_specs=(P(COL, ROW), P(None, None, None, None, AXES, None)),
        check_vma=False,
    )
```

```python
import jax
import jax.numpy as jnp
from jax import lax
from jax.sharding import Mesh
from jax.sharding import PartitionSpec as P

CTX = 16384
CAP = 32
SHORT = 256
ROW = ("xl", "core")
COL = ("y", "xh", "z")
AXES = ROW + COL


def row_order(x, dim):
    shape = x.shape
    quarter = shape[dim] // 4
    split = x.reshape(shape[:dim] + (2, 2, quarter) + shape[dim + 1 :])
    return jnp.swapaxes(split, dim, dim + 1).reshape(shape)


def swap_gather(x, name, index):
    other = lax.ppermute(x, name, perm=[(0, 1), (1, 0)])
    return jnp.where(
        index == 0, jnp.concatenate([x, other], axis=-1), jnp.concatenate([other, x], axis=-1)
    )


def swap_reduce(x, name, index, dim):
    block = x.shape[dim] // 2
    keep = lax.dynamic_slice_in_dim(x, index * block, block, axis=dim)
    give = lax.dynamic_slice_in_dim(x, (1 - index) * block, block, axis=dim)
    got = lax.ppermute(give, name, perm=[(0, 1), (1, 0)])
    return keep.astype(jnp.float32) + got.astype(jnp.float32)


def local(
    tokens,
    router,
    expert_ids,
    expert_in,
    expert_out,
    shared_in,
    shared_out,
    kv_cache,
    lengths,
    kv_proj,
    row_count,
    col_count,
):
    row_index = lax.axis_index(ROW)
    col_index = lax.axis_index(COL)
    core_index = lax.axis_index("core")
    tok_rows = tokens.shape[0]
    slice_width = tokens.shape[1]
    xl_index = lax.axis_index("xl")
    gathered = swap_gather(tokens, "core", core_index)
    gathered = swap_gather(gathered, "xl", xl_index)
    width = gathered.shape[1]
    half_width = width // 2
    tokens_f = gathered.astype(jnp.float32)
    normed = (
        tokens_f * lax.rsqrt(jnp.mean(tokens_f * tokens_f, axis=-1, keepdims=True) + 1e-06)
    ).astype(jnp.bfloat16)
    logits = jnp.dot(normed, router, preferred_element_type=jnp.float32)
    expert_total = router.shape[1]
    top_count = expert_ids.shape[1]
    catalog = jnp.arange(expert_total, dtype=jnp.int32)
    matches = expert_ids[:, :, None] == catalog
    picked = jnp.sum(jnp.where(matches, logits[:, None, :], 0.0), axis=2)
    sigmoids = jax.nn.sigmoid(picked)
    gate_weights = sigmoids / jnp.sum(sigmoids, axis=1, keepdims=True)
    flat_ids = expert_ids.reshape(-1)
    pair_count = flat_ids.shape[0]
    onehot = (flat_ids[:, None] == catalog).astype(jnp.bfloat16)
    pair_iota = jnp.arange(pair_count, dtype=jnp.int32)
    earlier = (pair_iota[None, :] < pair_iota[:, None]).astype(jnp.bfloat16)
    before = jnp.dot(earlier, onehot, preferred_element_type=jnp.float32)
    slot_index = jnp.sum(before * onehot.astype(jnp.float32), axis=1).astype(jnp.int32)
    dest_index = flat_ids * CAP + slot_index
    slot_total = expert_total * CAP
    slots = jnp.arange(slot_total, dtype=jnp.int32)
    dest_tok = dest_index.reshape(tok_rows, top_count)
    select_tok = jnp.any(dest_tok[None, :, :] == slots[:, None, None], axis=2).astype(jnp.bfloat16)
    layers, pairs, requests, _, slab_len, head_slice = kv_cache.shape
    device_total = row_count * col_count
    piece_len = slab_len // device_total
    span_local = jnp.einsum(
        "td,dph->tph", normed, kv_proj, preferred_element_type=jnp.float32
    ).astype(jnp.bfloat16)
    first_pos = CTX - tok_rows * col_count
    blocks_per_slab = slab_len // tok_rows
    first_span_slab = first_pos // slab_len
    span_pih = span_local.transpose(1, 0, 2)
    span_parts = []
    for part in range(blocks_per_slab):
        perm = [
            (b, first_span_slab + b // blocks_per_slab)
            for b in range(col_count)
            if b % blocks_per_slab == part
        ]
        span_parts.append(lax.ppermute(span_pih, COL, perm=perm))
    span_slab = jnp.concatenate(span_parts, axis=1)
    request_ids = jnp.arange(requests, dtype=jnp.int32)
    long_id = jnp.min(jnp.where(lengths == CTX, request_ids, requests))
    short_id = requests - 1 - long_id
    slab_data = kv_cache[:, :, :, 0]
    long_local = lax.dynamic_index_in_dim(slab_data, long_id, axis=2, keepdims=False)
    short_local = lax.dynamic_index_in_dim(slab_data, short_id, axis=2, keepdims=False)
    last_layer = jnp.where(col_index >= first_span_slab, span_slab, long_local[layers - 1])
    payload = jnp.concatenate([long_local[: layers - 1], last_layer[None]], axis=0)
    payload = payload.reshape(layers * pairs, device_total, piece_len, head_slice)
    local_experts = expert_total // col_count
    own_half = lax.dynamic_slice_in_dim(normed, core_index * half_width, half_width, axis=1)
    outgoing = jnp.dot(select_tok, own_half, preferred_element_type=jnp.float32)
    outgoing = outgoing.astype(jnp.bfloat16).reshape(col_count, local_experts, CAP, half_width)
    short_rows = SHORT // (col_count * piece_len)
    short_head = short_local[:, :, :SHORT].reshape(
        layers * pairs, short_rows, col_count, piece_len, head_slice
    )
    short_head = short_head.transpose(2, 0, 1, 3, 4).reshape(col_count, -1)
    dispatch_size = local_experts * CAP * half_width
    merged = jnp.concatenate([outgoing.reshape(col_count, -1), short_head], axis=1)
    merged = lax.all_to_all(merged, COL, split_axis=0, concat_axis=0, tiled=True)
    incoming_own = merged[:, :dispatch_size].reshape(col_count, local_experts, CAP, half_width)
    incoming_own = incoming_own.transpose(1, 0, 2, 3)
    short_cols = merged[0, dispatch_size:].reshape(
        layers * pairs, short_rows, piece_len, head_slice
    )
    incoming_other = lax.ppermute(incoming_own, "core", perm=[(0, 1), (1, 0)])
    weights_own = lax.dynamic_slice_in_dim(expert_in, core_index * half_width, half_width, axis=2)
    weights_other = lax.dynamic_slice_in_dim(
        expert_in, (1 - core_index) * half_width, half_width, axis=2
    )
    gate_up = jnp.einsum(
        "escd,egdf->gescf", incoming_own, weights_own, preferred_element_type=jnp.float32
    ) + jnp.einsum(
        "escd,egdf->gescf", incoming_other, weights_other, preferred_element_type=jnp.float32
    )
    hidden = (jax.nn.silu(gate_up[0]) * gate_up[1]).astype(jnp.bfloat16)
    quarter_parts = [
        jnp.einsum(
            "escf,efd->secd",
            hidden,
            expert_out[:, :, q * slice_width : (q + 1) * slice_width],
            preferred_element_type=jnp.float32,
        ).astype(jnp.bfloat16)
        for q in range(4)
    ]
    on_first = core_index == 0
    keep = jnp.stack(
        [
            jnp.where(on_first, quarter_parts[0], quarter_parts[1]),
            jnp.where(on_first, quarter_parts[2], quarter_parts[3]),
        ]
    )
    give = jnp.stack(
        [
            jnp.where(on_first, quarter_parts[1], quarter_parts[0]),
            jnp.where(on_first, quarter_parts[3], quarter_parts[2]),
        ]
    )
    got = lax.ppermute(give, "core", perm=[(0, 1), (1, 0)])
    chip_sum = (keep.astype(jnp.float32) + got.astype(jnp.float32)).astype(jnp.bfloat16)
    send = chip_sum.reshape(2 * col_count, -1)
    return_size = send.shape[1]
    relay = payload.reshape(layers * pairs, 2, 2, col_count, piece_len, head_slice)
    relay_keep = lax.dynamic_index_in_dim(relay, core_index, axis=2, keepdims=False)
    relay_give = lax.dynamic_index_in_dim(relay, 1 - core_index, axis=2, keepdims=False)
    relay_got = lax.ppermute(relay_give, "core", perm=[(0, 1), (1, 0)])
    relay_chip = jnp.where(
        on_first,
        jnp.stack([relay_keep, relay_got], axis=4),
        jnp.stack([relay_got, relay_keep], axis=4),
    )
    relay_chip = relay_chip.transpose(1, 2, 0, 3, 4, 5).reshape(2 * col_count, -1)
    merged_back = jnp.concatenate([send, relay_chip], axis=1)
    merged_back = lax.all_to_all(
        merged_back, ("xl",) + COL, split_axis=0, concat_axis=0, tiled=True
    )
    both = merged_back[:, :return_size]
    both = both.astype(jnp.float32).reshape(2, slot_total, slice_width)
    relaid = merged_back[:, return_size:].reshape(
        2, col_count, layers * pairs, piece_len, 2, head_slice
    )
    returned = (both[0] + both[1]).astype(jnp.bfloat16)
    pick = (dest_index[:, None] == slots[None, :]).astype(jnp.bfloat16)
    routed = jnp.dot(pick, returned, preferred_element_type=jnp.float32)
    routed = routed.reshape(tok_rows, top_count, slice_width)
    routed_sum = jnp.sum(gate_weights[:, :, None] * routed, axis=1)
    stacked = jnp.concatenate(
        [shared_in.transpose(1, 0, 2), shared_out.T[:, None, :]], axis=1
    )
    shared_full = lax.all_gather(stacked, COL, axis=0, tiled=True)
    shared_acc = jnp.einsum(
        "td,dgs->gts", normed, shared_full[:, 0:2, :], preferred_element_type=jnp.float32
    )
    shared_hidden = (jax.nn.silu(shared_acc[0]) * shared_acc[1]).astype(jnp.bfloat16)
    shared_terms = jnp.einsum(
        "ts,ds->td", shared_hidden, shared_full[:, 2, :], preferred_element_type=jnp.float32
    )
    shared_terms = row_order(shared_terms, 1)
    shared_half = swap_reduce(shared_terms.astype(jnp.bfloat16), "core", core_index, 1)
    shared_part = swap_reduce(shared_half.astype(jnp.bfloat16), "xl", xl_index, 1)
    mixed_out = (shared_part + routed_sum).astype(jnp.bfloat16)
    long_out = relaid.transpose(2, 1, 3, 0, 4, 5).reshape(
        layers, pairs, col_count, piece_len, row_count * head_slice
    )
    short_cols = jnp.concatenate(
        [
            short_cols,
            jnp.zeros(
                (layers * pairs, row_count - short_rows, piece_len, head_slice), jnp.bfloat16
            ),
        ],
        axis=1,
    )
    short_piece = lax.all_to_all(short_cols, ROW, split_axis=1, concat_axis=0, tiled=False)
    short_piece = short_piece.transpose(1, 2, 0, 3).reshape(
        layers, pairs, piece_len, row_count * head_slice
    )
    positions = (row_index * col_count + col_index) * piece_len + jnp.arange(
        piece_len, dtype=jnp.int32
    )
    short_live = positions < lengths[short_id]
    slab_ids = jnp.arange(col_count, dtype=jnp.int32)
    short_keep = (slab_ids[:, None] == 0) & short_live[None, :]
    short_out = jnp.where(
        short_keep[None, None, :, :, None], short_piece[:, :, None], jnp.zeros((), jnp.bfloat16)
    )
    cache_out = jnp.where(
        (request_ids == long_id)[None, None, :, None, None, None],
        long_out[:, :, None],
        short_out[:, :, None],
    )
    return (mixed_out, cache_out)


def solution(mesh):
    row_count = mesh.shape["row"]
    col_count = mesh.shape["col"]
    fine = Mesh(mesh.devices.reshape(2, row_count // 2, 4, 2, col_count // 8), AXES)

    def body(*args):
        return local(*args, row_count, col_count)

    return jax.shard_map(
        body,
        mesh=fine,
        in_specs=(
            P(COL, ROW),
            P(),
            P(COL, None),
            P(COL, None, None, ROW),
            P(COL, ROW, None),
            P(None, COL, ROW),
            P(ROW, COL),
            P(None, None, None, COL, None, ROW),
            P(),
            P(None, None, ROW),
        ),
        out_specs=(P(COL, ROW), P(None, None, None, None, AXES, None)),
        check_vma=False,
    )
```

```python
import jax
import jax.numpy as jnp
from jax import lax
from jax.sharding import Mesh
from jax.sharding import PartitionSpec as P

CTX = 16384
CAP = 32
SHORT = 256
ROW = ("xl", "core")
COL = ("y", "xh", "z")
AXES = ROW + COL


def row_order(x, dim):
    shape = x.shape
    quarter = shape[dim] // 4
    split = x.reshape(shape[:dim] + (2, 2, quarter) + shape[dim + 1 :])
    return jnp.swapaxes(split, dim, dim + 1).reshape(shape)


def swap_gather(x, name, index):
    other = lax.ppermute(x, name, perm=[(0, 1), (1, 0)])
    return jnp.where(
        index == 0, jnp.concatenate([x, other], axis=-1), jnp.concatenate([other, x], axis=-1)
    )


def swap_reduce(x, name, index, dim):
    block = x.shape[dim] // 2
    keep = lax.dynamic_slice_in_dim(x, index * block, block, axis=dim)
    give = lax.dynamic_slice_in_dim(x, (1 - index) * block, block, axis=dim)
    got = lax.ppermute(give, name, perm=[(0, 1), (1, 0)])
    return keep.astype(jnp.float32) + got.astype(jnp.float32)


def local(
    tokens,
    router,
    expert_ids,
    expert_in,
    expert_out,
    shared_in,
    shared_out,
    kv_cache,
    lengths,
    kv_proj,
    row_count,
    col_count,
):
    row_index = lax.axis_index(ROW)
    col_index = lax.axis_index(COL)
    core_index = lax.axis_index("core")
    tok_rows = tokens.shape[0]
    slice_width = tokens.shape[1]
    xl_index = lax.axis_index("xl")
    gathered = swap_gather(tokens, "core", core_index)
    gathered = swap_gather(gathered, "xl", xl_index)
    width = gathered.shape[1]
    half_width = width // 2
    tokens_f = gathered.astype(jnp.float32)
    normed = (
        tokens_f * lax.rsqrt(jnp.mean(tokens_f * tokens_f, axis=-1, keepdims=True) + 1e-06)
    ).astype(jnp.bfloat16)
    logits = jnp.dot(normed, router, preferred_element_type=jnp.float32)
    expert_total = router.shape[1]
    top_count = expert_ids.shape[1]
    catalog = jnp.arange(expert_total, dtype=jnp.int32)
    matches = expert_ids[:, :, None] == catalog
    picked = jnp.sum(jnp.where(matches, logits[:, None, :], 0.0), axis=2)
    sigmoids = jax.nn.sigmoid(picked)
    gate_weights = sigmoids / jnp.sum(sigmoids, axis=1, keepdims=True)
    flat_ids = expert_ids.reshape(-1)
    pair_count = flat_ids.shape[0]
    onehot = (flat_ids[:, None] == catalog).astype(jnp.bfloat16)
    pair_iota = jnp.arange(pair_count, dtype=jnp.int32)
    earlier = (pair_iota[None, :] < pair_iota[:, None]).astype(jnp.bfloat16)
    before = jnp.dot(earlier, onehot, preferred_element_type=jnp.float32)
    slot_index = jnp.sum(before * onehot.astype(jnp.float32), axis=1).astype(jnp.int32)
    dest_index = flat_ids * CAP + slot_index
    slot_total = expert_total * CAP
    slots = jnp.arange(slot_total, dtype=jnp.int32)
    dest_tok = dest_index.reshape(tok_rows, top_count)
    select_tok = jnp.any(dest_tok[None, :, :] == slots[:, None, None], axis=2).astype(jnp.bfloat16)
    local_experts = expert_total // col_count
    own_half = lax.dynamic_slice_in_dim(normed, core_index * half_width, half_width, axis=1)
    outgoing = jnp.dot(select_tok, own_half, preferred_element_type=jnp.float32)
    outgoing = outgoing.astype(jnp.bfloat16).reshape(col_count, local_experts, CAP, half_width)
    incoming_own = lax.all_to_all(outgoing, COL, split_axis=0, concat_axis=1, tiled=False)
    incoming_other = lax.ppermute(incoming_own, "core", perm=[(0, 1), (1, 0)])
    weights_own = lax.dynamic_slice_in_dim(expert_in, core_index * half_width, half_width, axis=2)
    weights_other = lax.dynamic_slice_in_dim(
        expert_in, (1 - core_index) * half_width, half_width, axis=2
    )
    gate_up = jnp.einsum(
        "escd,egdf->gescf", incoming_own, weights_own, preferred_element_type=jnp.float32
    ) + jnp.einsum(
        "escd,egdf->gescf", incoming_other, weights_other, preferred_element_type=jnp.float32
    )
    hidden = (jax.nn.silu(gate_up[0]) * gate_up[1]).astype(jnp.bfloat16)
    quarter_parts = [
        jnp.einsum(
            "escf,efd->secd",
            hidden,
            expert_out[:, :, q * slice_width : (q + 1) * slice_width],
            preferred_element_type=jnp.float32,
        ).astype(jnp.bfloat16)
        for q in range(4)
    ]
    on_first = core_index == 0
    keep = jnp.stack(
        [
            jnp.where(on_first, quarter_parts[0], quarter_parts[1]),
            jnp.where(on_first, quarter_parts[2], quarter_parts[3]),
        ]
    )
    give = jnp.stack(
        [
            jnp.where(on_first, quarter_parts[1], quarter_parts[0]),
            jnp.where(on_first, quarter_parts[3], quarter_parts[2]),
        ]
    )
    got = lax.ppermute(give, "core", perm=[(0, 1), (1, 0)])
    chip_sum = (keep.astype(jnp.float32) + got.astype(jnp.float32)).astype(jnp.bfloat16)
    send = chip_sum.reshape(2 * col_count, local_experts * CAP, slice_width)
    both = lax.all_to_all(send, ("xl",) + COL, split_axis=0, concat_axis=0, tiled=True)
    both = both.astype(jnp.float32).reshape(2, slot_total, slice_width)
    returned = (both[0] + both[1]).astype(jnp.bfloat16)
    pick = (dest_index[:, None] == slots[None, :]).astype(jnp.bfloat16)
    routed = jnp.dot(pick, returned, preferred_element_type=jnp.float32)
    routed = routed.reshape(tok_rows, top_count, slice_width)
    routed_sum = jnp.sum(gate_weights[:, :, None] * routed, axis=1)
    stacked = jnp.concatenate(
        [shared_in.transpose(1, 0, 2), shared_out.T[:, None, :]], axis=1
    )
    shared_full = lax.all_gather(stacked, COL, axis=0, tiled=True)
    shared_acc = jnp.einsum(
        "td,dgs->gts", normed, shared_full[:, 0:2, :], preferred_element_type=jnp.float32
    )
    shared_hidden = (jax.nn.silu(shared_acc[0]) * shared_acc[1]).astype(jnp.bfloat16)
    shared_terms = jnp.einsum(
        "ts,ds->td", shared_hidden, shared_full[:, 2, :], preferred_element_type=jnp.float32
    )
    shared_terms = row_order(shared_terms, 1)
    shared_half = swap_reduce(shared_terms.astype(jnp.bfloat16), "core", core_index, 1)
    shared_part = swap_reduce(shared_half.astype(jnp.bfloat16), "xl", xl_index, 1)
    mixed_out = (shared_part + routed_sum).astype(jnp.bfloat16)
    layers, pairs, requests, _, slab_len, head_slice = kv_cache.shape
    device_total = row_count * col_count
    piece_len = slab_len // device_total
    span_local = jnp.einsum(
        "td,dph->tph", normed, kv_proj, preferred_element_type=jnp.float32
    ).astype(jnp.bfloat16)
    first_pos = CTX - tok_rows * col_count
    blocks_per_slab = slab_len // tok_rows
    first_span_slab = first_pos // slab_len
    span_pih = span_local.transpose(1, 0, 2)
    span_parts = []
    for part in range(blocks_per_slab):
        perm = [
            (b, first_span_slab + b // blocks_per_slab)
            for b in range(col_count)
            if b % blocks_per_slab == part
        ]
        span_parts.append(lax.ppermute(span_pih, COL, perm=perm))
    span_slab = jnp.concatenate(span_parts, axis=1)
    request_ids = jnp.arange(requests, dtype=jnp.int32)
    long_id = jnp.min(jnp.where(lengths == CTX, request_ids, requests))
    short_id = requests - 1 - long_id
    slab_data = kv_cache[:, :, :, 0]
    long_local = lax.dynamic_index_in_dim(slab_data, long_id, axis=2, keepdims=False)
    short_local = lax.dynamic_index_in_dim(slab_data, short_id, axis=2, keepdims=False)
    last_layer = jnp.where(col_index >= first_span_slab, span_slab, long_local[layers - 1])
    payload = jnp.concatenate([long_local[: layers - 1], last_layer[None]], axis=0)
    payload = payload.reshape(layers * pairs, device_total, piece_len, head_slice)
    relaid = lax.all_to_all(payload, AXES, split_axis=1, concat_axis=0, tiled=False)
    long_out = relaid.reshape(row_count, col_count, layers, pairs, piece_len, head_slice)
    long_out = long_out.transpose(2, 3, 1, 4, 0, 5).reshape(
        layers, pairs, col_count, piece_len, row_count * head_slice
    )
    short_rows = SHORT // (col_count * piece_len)
    short_head = short_local[:, :, :SHORT].reshape(
        layers * pairs, short_rows, col_count, piece_len, head_slice
    )
    held = short_head.transpose(2, 0, 1, 3, 4)
    stride = col_count // 2
    while stride >= 1:
        perm = [(c, c + stride) for c in range(0, col_count, 2 * stride)]
        moved = lax.ppermute(held[stride : 2 * stride], COL, perm=perm)
        held = jnp.where(col_index % (2 * stride) == 0, held[:stride], moved)
        stride //= 2
    short_cols = held[0]
    by_source = []
    for shift in range(row_count):
        target = (row_index + shift) % row_count
        part = lax.dynamic_index_in_dim(
            short_cols, jnp.minimum(target, short_rows - 1), axis=1, keepdims=False
        )
        part = jnp.where(target < short_rows, part, jnp.zeros_like(part))
        if shift > 0:
            part = lax.ppermute(
                part, ROW, perm=[(r, (r + shift) % row_count) for r in range(row_count)]
            )
        by_source.append(part)
    sources = (row_index - jnp.arange(row_count, dtype=jnp.int32)) % row_count
    order = jnp.argsort(sources)
    short_piece = jnp.take(jnp.stack(by_source, axis=0), order, axis=0)
    short_piece = short_piece.transpose(1, 2, 0, 3).reshape(
        layers, pairs, piece_len, row_count * head_slice
    )
    positions = (row_index * col_count + col_index) * piece_len + jnp.arange(
        piece_len, dtype=jnp.int32
    )
    short_live = positions < lengths[short_id]
    slab_ids = jnp.arange(col_count, dtype=jnp.int32)
    short_keep = (slab_ids[:, None] == 0) & short_live[None, :]
    short_out = jnp.where(
        short_keep[None, None, :, :, None], short_piece[:, :, None], jnp.zeros((), jnp.bfloat16)
    )
    cache_out = jnp.where(
        (request_ids == long_id)[None, None, :, None, None, None],
        long_out[:, :, None],
        short_out[:, :, None],
    )
    return (mixed_out, cache_out)


def solution(mesh):
    row_count = mesh.shape["row"]
    col_count = mesh.shape["col"]
    fine = Mesh(mesh.devices.reshape(2, row_count // 2, 4, 2, col_count // 8), AXES)

    def body(*args):
        return local(*args, row_count, col_count)

    return jax.shard_map(
        body,
        mesh=fine,
        in_specs=(
            P(COL, ROW),
            P(),
            P(COL, None),
            P(COL, None, None, ROW),
            P(COL, ROW, None),
            P(None, COL, ROW),
            P(ROW, COL),
            P(None, None, None, COL, None, ROW),
            P(),
            P(None, None, ROW),
        ),
        out_specs=(P(COL, ROW), P(None, None, None, None, AXES, None)),
        check_vma=False,
    )
```

```python
import jax
import jax.numpy as jnp
from jax import lax
from jax.sharding import Mesh
from jax.sharding import PartitionSpec as P

CTX = 16384
CAP = 32
ROW = ("xl", "core")
COL = ("y", "xh", "z")
AXES = ROW + COL


def relay_slabs(chosen, row_count, col_count):
    layers = chosen.shape[0]
    pairs = chosen.shape[1]
    requests = chosen.shape[2]
    slab_len = chosen.shape[4]
    head_width = chosen.shape[5]
    groups = layers * pairs * requests
    sectioned = chosen.reshape(groups, 1, slab_len, head_width)
    piece_len = slab_len // (row_count * col_count)
    relaid = lax.all_to_all(sectioned, AXES, split_axis=2, concat_axis=1, tiled=True)
    relaid = relaid.reshape(groups, row_count, col_count, piece_len, head_width)
    relaid = relaid.transpose(0, 2, 3, 1, 4).reshape(
        groups, col_count, piece_len, row_count * head_width
    )
    return relaid.reshape(layers, pairs, requests, col_count, piece_len, row_count * head_width)


def row_order(x, dim):
    shape = x.shape
    quarter = shape[dim] // 4
    split = x.reshape(shape[:dim] + (2, 2, quarter) + shape[dim + 1 :])
    return jnp.swapaxes(split, dim, dim + 1).reshape(shape)


def swap_gather(x, name, index):
    other = lax.ppermute(x, name, perm=[(0, 1), (1, 0)])
    return jnp.where(
        index == 0, jnp.concatenate([x, other], axis=-1), jnp.concatenate([other, x], axis=-1)
    )


def swap_reduce(x, name, index, dim):
    block = x.shape[dim] // 2
    keep = lax.dynamic_slice_in_dim(x, index * block, block, axis=dim)
    give = lax.dynamic_slice_in_dim(x, (1 - index) * block, block, axis=dim)
    got = lax.ppermute(give, name, perm=[(0, 1), (1, 0)])
    return keep.astype(jnp.float32) + got.astype(jnp.float32)


def local(
    tokens,
    router,
    expert_ids,
    expert_in,
    expert_out,
    shared_in,
    shared_out,
    kv_cache,
    lengths,
    kv_proj,
    row_count,
    col_count,
):
    row_index = lax.axis_index(ROW)
    col_index = lax.axis_index(COL)
    core_index = lax.axis_index("core")
    tok_rows = tokens.shape[0]
    slice_width = tokens.shape[1]
    xl_index = lax.axis_index("xl")
    gathered = swap_gather(tokens, "core", core_index)
    gathered = swap_gather(gathered, "xl", xl_index)
    width = gathered.shape[1]
    half_width = width // 2
    tokens_f = gathered.astype(jnp.float32)
    normed = (
        tokens_f * lax.rsqrt(jnp.mean(tokens_f * tokens_f, axis=-1, keepdims=True) + 1e-06)
    ).astype(jnp.bfloat16)
    logits = jnp.dot(normed, router, preferred_element_type=jnp.float32)
    expert_total = router.shape[1]
    top_count = expert_ids.shape[1]
    catalog = jnp.arange(expert_total, dtype=jnp.int32)
    matches = expert_ids[:, :, None] == catalog
    picked = jnp.sum(jnp.where(matches, logits[:, None, :], 0.0), axis=2)
    sigmoids = jax.nn.sigmoid(picked)
    gate_weights = sigmoids / jnp.sum(sigmoids, axis=1, keepdims=True)
    flat_ids = expert_ids.reshape(-1)
    pair_count = flat_ids.shape[0]
    onehot = (flat_ids[:, None] == catalog).astype(jnp.bfloat16)
    pair_iota = jnp.arange(pair_count, dtype=jnp.int32)
    earlier = (pair_iota[None, :] < pair_iota[:, None]).astype(jnp.bfloat16)
    before = jnp.dot(earlier, onehot, preferred_element_type=jnp.float32)
    slot_index = jnp.sum(before * onehot.astype(jnp.float32), axis=1).astype(jnp.int32)
    dest_index = flat_ids * CAP + slot_index
    slot_total = expert_total * CAP
    slots = jnp.arange(slot_total, dtype=jnp.int32)
    dest_tok = dest_index.reshape(tok_rows, top_count)
    select_tok = jnp.any(dest_tok[None, :, :] == slots[:, None, None], axis=2).astype(jnp.bfloat16)
    local_experts = expert_total // col_count
    own_half = lax.dynamic_slice_in_dim(normed, core_index * half_width, half_width, axis=1)
    outgoing = jnp.dot(select_tok, own_half, preferred_element_type=jnp.float32)
    outgoing = outgoing.astype(jnp.bfloat16).reshape(col_count, local_experts, CAP, half_width)
    relaid = relay_slabs(kv_cache, row_count, col_count)
    outgoing, relaid = lax.optimization_barrier((outgoing, relaid))
    incoming_own = lax.all_to_all(outgoing, COL, split_axis=0, concat_axis=1, tiled=False)
    incoming_other = lax.ppermute(incoming_own, "core", perm=[(0, 1), (1, 0)])
    weights_own = lax.dynamic_slice_in_dim(expert_in, core_index * half_width, half_width, axis=2)
    weights_other = lax.dynamic_slice_in_dim(
        expert_in, (1 - core_index) * half_width, half_width, axis=2
    )
    gate_up = jnp.einsum(
        "escd,egdf->gescf", incoming_own, weights_own, preferred_element_type=jnp.float32
    ) + jnp.einsum(
        "escd,egdf->gescf", incoming_other, weights_other, preferred_element_type=jnp.float32
    )
    hidden = (jax.nn.silu(gate_up[0]) * gate_up[1]).astype(jnp.bfloat16)
    quarter_parts = [
        jnp.einsum(
            "escf,efd->secd",
            hidden,
            expert_out[:, :, q * slice_width : (q + 1) * slice_width],
            preferred_element_type=jnp.float32,
        ).astype(jnp.bfloat16)
        for q in range(4)
    ]
    on_first = core_index == 0
    keep = jnp.stack(
        [
            jnp.where(on_first, quarter_parts[0], quarter_parts[1]),
            jnp.where(on_first, quarter_parts[2], quarter_parts[3]),
        ]
    )
    give = jnp.stack(
        [
            jnp.where(on_first, quarter_parts[1], quarter_parts[0]),
            jnp.where(on_first, quarter_parts[3], quarter_parts[2]),
        ]
    )
    got = lax.ppermute(give, "core", perm=[(0, 1), (1, 0)])
    chip_sum = (keep.astype(jnp.float32) + got.astype(jnp.float32)).astype(jnp.bfloat16)
    send = chip_sum.reshape(2 * col_count, local_experts * CAP, slice_width)
    both = lax.all_to_all(send, ("xl",) + COL, split_axis=0, concat_axis=0, tiled=True)
    both = both.astype(jnp.float32).reshape(2, slot_total, slice_width)
    returned = (both[0] + both[1]).astype(jnp.bfloat16)
    pick = (dest_index[:, None] == slots[None, :]).astype(jnp.bfloat16)
    routed = jnp.dot(pick, returned, preferred_element_type=jnp.float32)
    routed = routed.reshape(tok_rows, top_count, slice_width)
    routed_sum = jnp.sum(gate_weights[:, :, None] * routed, axis=1)
    stacked = jnp.concatenate(
        [shared_in.transpose(1, 0, 2), shared_out.T[:, None, :]], axis=1
    )
    shared_full = lax.all_gather(stacked, COL, axis=0, tiled=True)
    shared_acc = jnp.einsum(
        "td,dgs->gts", normed, shared_full[:, 0:2, :], preferred_element_type=jnp.float32
    )
    shared_hidden = (jax.nn.silu(shared_acc[0]) * shared_acc[1]).astype(jnp.bfloat16)
    shared_terms = jnp.einsum(
        "ts,ds->td", shared_hidden, shared_full[:, 2, :], preferred_element_type=jnp.float32
    )
    shared_terms = row_order(shared_terms, 1)
    shared_half = swap_reduce(shared_terms.astype(jnp.bfloat16), "core", core_index, 1)
    shared_part = swap_reduce(shared_half.astype(jnp.bfloat16), "xl", xl_index, 1)
    mixed_out = (shared_part + routed_sum).astype(jnp.bfloat16)
    layers = kv_cache.shape[0]
    pairs = kv_cache.shape[1]
    requests = kv_cache.shape[2]
    slab_len = kv_cache.shape[4]
    head_slice = kv_cache.shape[5]
    piece_len = slab_len // (row_count * col_count)
    device_total = row_count * col_count
    span_local = jnp.einsum(
        "td,dph->tph", normed, kv_proj, preferred_element_type=jnp.float32
    ).astype(jnp.bfloat16)
    first_pos = CTX - tok_rows * col_count
    send_offset = (first_pos + col_index * tok_rows) % slab_len
    outbound = lax.dynamic_update_slice(
        jnp.zeros((slab_len, pairs, head_slice), jnp.bfloat16), span_local, (send_offset, 0, 0)
    )
    outbound = outbound.reshape(device_total, piece_len, pairs, head_slice)
    inbound = lax.all_to_all(outbound, AXES, split_axis=0, concat_axis=0, tiled=True)
    inbound = inbound.reshape(row_count, col_count, piece_len, pairs, head_slice)
    device_flat = row_index * col_count + col_index
    source_block = jnp.arange(col_count, dtype=jnp.int32)[:, None]
    within = device_flat * piece_len + jnp.arange(piece_len, dtype=jnp.int32)[None, :]
    offset_tok = (within - first_pos - source_block * tok_rows) % slab_len
    usable = offset_tok < tok_rows
    slab_of = (first_pos + source_block * tok_rows + offset_tok) // slab_len
    slab_ids = jnp.arange(col_count, dtype=jnp.int32)[:, None, None]
    placing = ((slab_of[None, :, :] == slab_ids) & usable[None, :, :]).astype(jnp.bfloat16)
    placed = jnp.einsum("sck,rckph->pskrh", placing, inbound, preferred_element_type=jnp.float32)
    placed = placed.reshape(pairs, col_count, piece_len, row_count * head_slice).astype(
        jnp.bfloat16
    )
    covered = jnp.sum(placing.astype(jnp.float32), axis=1) > 0.5
    first_long = jnp.min(jnp.where(lengths == CTX, jnp.arange(requests, dtype=jnp.int32), requests))
    start_pos = (row_index * col_count + col_index) * piece_len
    places = (
        jnp.arange(col_count, dtype=jnp.int32)[:, None] * slab_len
        + start_pos
        + jnp.arange(piece_len, dtype=jnp.int32)[None, :]
    )
    live_mask = places[None, :, :] < lengths[:, None, None]
    cache_out = jnp.where(live_mask[None, None, :, :, :, None], relaid, jnp.zeros((), relaid.dtype))
    layer_pick = (jnp.arange(layers, dtype=jnp.int32) == layers - 1)[
        :, None, None, None, None, None
    ]
    request_pick = (jnp.arange(requests, dtype=jnp.int32) == first_long)[
        None, None, :, None, None, None
    ]
    select = layer_pick & request_pick & covered[None, None, None, :, :, None]
    cache_out = jnp.where(select, placed[None, :, None], cache_out)
    return (mixed_out, cache_out)


def solution(mesh):
    row_count = mesh.shape["row"]
    col_count = mesh.shape["col"]
    fine = Mesh(mesh.devices.reshape(2, row_count // 2, 4, 2, col_count // 8), AXES)

    def body(*args):
        return local(*args, row_count, col_count)

    return jax.shard_map(
        body,
        mesh=fine,
        in_specs=(
            P(COL, ROW),
            P(),
            P(COL, None),
            P(COL, None, None, ROW),
            P(COL, ROW, None),
            P(None, COL, ROW),
            P(ROW, COL),
            P(None, None, None, COL, None, ROW),
            P(),
            P(None, None, ROW),
        ),
        out_specs=(P(COL, ROW), P(None, None, None, None, AXES, None)),
        check_vma=False,
    )
```

```python
import jax
import jax.numpy as jnp
from jax import lax
from jax.sharding import Mesh
from jax.sharding import PartitionSpec as P

CTX = 16384
CAP = 32
ROW = ("xl", "core")
COL = ("y", "xh", "z")
AXES = ROW + COL


def relay_slabs(chosen, row_count, col_count):
    layers = chosen.shape[0]
    pairs = chosen.shape[1]
    requests = chosen.shape[2]
    slab_len = chosen.shape[4]
    head_width = chosen.shape[5]
    groups = layers * pairs * requests
    sectioned = chosen.reshape(groups, 1, slab_len, head_width)
    piece_len = slab_len // (row_count * col_count)
    relaid = lax.all_to_all(sectioned, AXES, split_axis=2, concat_axis=1, tiled=True)
    relaid = relaid.reshape(groups, row_count, col_count, piece_len, head_width)
    relaid = relaid.transpose(0, 2, 3, 1, 4).reshape(
        groups, col_count, piece_len, row_count * head_width
    )
    return relaid.reshape(layers, pairs, requests, col_count, piece_len, row_count * head_width)


def row_order(x, dim):
    shape = x.shape
    quarter = shape[dim] // 4
    split = x.reshape(shape[:dim] + (2, 2, quarter) + shape[dim + 1 :])
    return jnp.swapaxes(split, dim, dim + 1).reshape(shape)


def swap_gather(x, name, index):
    other = lax.ppermute(x, name, perm=[(0, 1), (1, 0)])
    return jnp.where(
        index == 0, jnp.concatenate([x, other], axis=-1), jnp.concatenate([other, x], axis=-1)
    )


def swap_reduce(x, name, index, dim):
    block = x.shape[dim] // 2
    keep = lax.dynamic_slice_in_dim(x, index * block, block, axis=dim)
    give = lax.dynamic_slice_in_dim(x, (1 - index) * block, block, axis=dim)
    got = lax.ppermute(give, name, perm=[(0, 1), (1, 0)])
    return keep.astype(jnp.float32) + got.astype(jnp.float32)


def local(
    tokens,
    router,
    expert_ids,
    expert_in,
    expert_out,
    shared_in,
    shared_out,
    kv_cache,
    lengths,
    kv_proj,
    row_count,
    col_count,
):
    row_index = lax.axis_index(ROW)
    col_index = lax.axis_index(COL)
    core_index = lax.axis_index("core")
    tok_rows = tokens.shape[0]
    slice_width = tokens.shape[1]
    xl_index = lax.axis_index("xl")
    gathered = swap_gather(tokens, "core", core_index)
    gathered = swap_gather(gathered, "xl", xl_index)
    width = gathered.shape[1]
    half_width = width // 2
    tokens_f = gathered.astype(jnp.float32)
    normed = (
        tokens_f * lax.rsqrt(jnp.mean(tokens_f * tokens_f, axis=-1, keepdims=True) + 1e-06)
    ).astype(jnp.bfloat16)
    logits = jnp.dot(normed, router, preferred_element_type=jnp.float32)
    expert_total = router.shape[1]
    top_count = expert_ids.shape[1]
    catalog = jnp.arange(expert_total, dtype=jnp.int32)
    matches = expert_ids[:, :, None] == catalog
    picked = jnp.sum(jnp.where(matches, logits[:, None, :], 0.0), axis=2)
    sigmoids = jax.nn.sigmoid(picked)
    gate_weights = sigmoids / jnp.sum(sigmoids, axis=1, keepdims=True)
    flat_ids = expert_ids.reshape(-1)
    pair_count = flat_ids.shape[0]
    onehot = (flat_ids[:, None] == catalog).astype(jnp.bfloat16)
    pair_iota = jnp.arange(pair_count, dtype=jnp.int32)
    earlier = (pair_iota[None, :] < pair_iota[:, None]).astype(jnp.bfloat16)
    before = jnp.dot(earlier, onehot, preferred_element_type=jnp.float32)
    slot_index = jnp.sum(before * onehot.astype(jnp.float32), axis=1).astype(jnp.int32)
    dest_index = flat_ids * CAP + slot_index
    slot_total = expert_total * CAP
    slots = jnp.arange(slot_total, dtype=jnp.int32)
    dest_tok = dest_index.reshape(tok_rows, top_count)
    select_tok = jnp.any(dest_tok[None, :, :] == slots[:, None, None], axis=2).astype(jnp.bfloat16)
    local_experts = expert_total // col_count
    own_half = lax.dynamic_slice_in_dim(normed, core_index * half_width, half_width, axis=1)
    outgoing = jnp.dot(select_tok, own_half, preferred_element_type=jnp.float32)
    outgoing = outgoing.astype(jnp.bfloat16).reshape(col_count, local_experts, CAP, half_width)
    incoming_own = lax.all_to_all(outgoing, COL, split_axis=0, concat_axis=1, tiled=False)
    incoming_other = lax.ppermute(incoming_own, "core", perm=[(0, 1), (1, 0)])
    weights_own = lax.dynamic_slice_in_dim(expert_in, core_index * half_width, half_width, axis=2)
    weights_other = lax.dynamic_slice_in_dim(
        expert_in, (1 - core_index) * half_width, half_width, axis=2
    )
    gate_up = jnp.einsum(
        "escd,egdf->gescf", incoming_own, weights_own, preferred_element_type=jnp.float32
    ) + jnp.einsum(
        "escd,egdf->gescf", incoming_other, weights_other, preferred_element_type=jnp.float32
    )
    hidden = (jax.nn.silu(gate_up[0]) * gate_up[1]).astype(jnp.bfloat16)
    quarter_parts = [
        jnp.einsum(
            "escf,efd->secd",
            hidden,
            expert_out[:, :, q * slice_width : (q + 1) * slice_width],
            preferred_element_type=jnp.float32,
        ).astype(jnp.bfloat16)
        for q in range(4)
    ]
    on_first = core_index == 0
    keep = jnp.stack(
        [
            jnp.where(on_first, quarter_parts[0], quarter_parts[1]),
            jnp.where(on_first, quarter_parts[2], quarter_parts[3]),
        ]
    )
    give = jnp.stack(
        [
            jnp.where(on_first, quarter_parts[1], quarter_parts[0]),
            jnp.where(on_first, quarter_parts[3], quarter_parts[2]),
        ]
    )
    got = lax.ppermute(give, "core", perm=[(0, 1), (1, 0)])
    chip_sum = (keep.astype(jnp.float32) + got.astype(jnp.float32)).astype(jnp.bfloat16)
    send = chip_sum.reshape(2 * col_count, local_experts * CAP, slice_width)
    both = lax.all_to_all(send, ("xl",) + COL, split_axis=0, concat_axis=0, tiled=True)
    both, kv_cache = lax.optimization_barrier((both, kv_cache))
    both = both.astype(jnp.float32).reshape(2, slot_total, slice_width)
    returned = (both[0] + both[1]).astype(jnp.bfloat16)
    pick = (dest_index[:, None] == slots[None, :]).astype(jnp.bfloat16)
    routed = jnp.dot(pick, returned, preferred_element_type=jnp.float32)
    routed = routed.reshape(tok_rows, top_count, slice_width)
    routed_sum = jnp.sum(gate_weights[:, :, None] * routed, axis=1)
    stacked = jnp.concatenate(
        [shared_in.transpose(1, 0, 2), shared_out.T[:, None, :]], axis=1
    )
    shared_full = lax.all_gather(stacked, COL, axis=0, tiled=True)
    shared_acc = jnp.einsum(
        "td,dgs->gts", normed, shared_full[:, 0:2, :], preferred_element_type=jnp.float32
    )
    shared_hidden = (jax.nn.silu(shared_acc[0]) * shared_acc[1]).astype(jnp.bfloat16)
    shared_terms = jnp.einsum(
        "ts,ds->td", shared_hidden, shared_full[:, 2, :], preferred_element_type=jnp.float32
    )
    shared_terms = row_order(shared_terms, 1)
    shared_half = swap_reduce(shared_terms.astype(jnp.bfloat16), "core", core_index, 1)
    shared_part = swap_reduce(shared_half.astype(jnp.bfloat16), "xl", xl_index, 1)
    mixed_out = (shared_part + routed_sum).astype(jnp.bfloat16)
    layers = kv_cache.shape[0]
    pairs = kv_cache.shape[1]
    requests = kv_cache.shape[2]
    slab_len = kv_cache.shape[4]
    head_slice = kv_cache.shape[5]
    piece_len = slab_len // (row_count * col_count)
    device_total = row_count * col_count
    span_local = jnp.einsum(
        "td,dph->tph", normed, kv_proj, preferred_element_type=jnp.float32
    ).astype(jnp.bfloat16)
    first_pos = CTX - tok_rows * col_count
    send_offset = (first_pos + col_index * tok_rows) % slab_len
    outbound = lax.dynamic_update_slice(
        jnp.zeros((slab_len, pairs, head_slice), jnp.bfloat16), span_local, (send_offset, 0, 0)
    )
    outbound = outbound.reshape(device_total, piece_len, pairs, head_slice)
    inbound = lax.all_to_all(outbound, AXES, split_axis=0, concat_axis=0, tiled=True)
    inbound = inbound.reshape(row_count, col_count, piece_len, pairs, head_slice)
    device_flat = row_index * col_count + col_index
    source_block = jnp.arange(col_count, dtype=jnp.int32)[:, None]
    within = device_flat * piece_len + jnp.arange(piece_len, dtype=jnp.int32)[None, :]
    offset_tok = (within - first_pos - source_block * tok_rows) % slab_len
    usable = offset_tok < tok_rows
    slab_of = (first_pos + source_block * tok_rows + offset_tok) // slab_len
    slab_ids = jnp.arange(col_count, dtype=jnp.int32)[:, None, None]
    placing = ((slab_of[None, :, :] == slab_ids) & usable[None, :, :]).astype(jnp.bfloat16)
    placed = jnp.einsum("sck,rckph->pskrh", placing, inbound, preferred_element_type=jnp.float32)
    placed = placed.reshape(pairs, col_count, piece_len, row_count * head_slice).astype(
        jnp.bfloat16
    )
    covered = jnp.sum(placing.astype(jnp.float32), axis=1) > 0.5
    first_long = jnp.min(jnp.where(lengths == CTX, jnp.arange(requests, dtype=jnp.int32), requests))
    relaid = relay_slabs(kv_cache, row_count, col_count)
    start_pos = (row_index * col_count + col_index) * piece_len
    places = (
        jnp.arange(col_count, dtype=jnp.int32)[:, None] * slab_len
        + start_pos
        + jnp.arange(piece_len, dtype=jnp.int32)[None, :]
    )
    live_mask = places[None, :, :] < lengths[:, None, None]
    cache_out = jnp.where(live_mask[None, None, :, :, :, None], relaid, jnp.zeros((), relaid.dtype))
    layer_pick = (jnp.arange(layers, dtype=jnp.int32) == layers - 1)[
        :, None, None, None, None, None
    ]
    request_pick = (jnp.arange(requests, dtype=jnp.int32) == first_long)[
        None, None, :, None, None, None
    ]
    select = layer_pick & request_pick & covered[None, None, None, :, :, None]
    cache_out = jnp.where(select, placed[None, :, None], cache_out)
    return (mixed_out, cache_out)


def solution(mesh):
    row_count = mesh.shape["row"]
    col_count = mesh.shape["col"]
    fine = Mesh(mesh.devices.reshape(2, row_count // 2, 4, 2, col_count // 8), AXES)

    def body(*args):
        return local(*args, row_count, col_count)

    return jax.shard_map(
        body,
        mesh=fine,
        in_specs=(
            P(COL, ROW),
            P(),
            P(COL, None),
            P(COL, None, None, ROW),
            P(COL, ROW, None),
            P(None, COL, ROW),
            P(ROW, COL),
            P(None, None, None, COL, None, ROW),
            P(),
            P(None, None, ROW),
        ),
        out_specs=(P(COL, ROW), P(None, None, None, None, AXES, None)),
        check_vma=False,
    )
```
